512 devices in a mesh: rows: 64 (over x, y, z_lo), feat: 8 (over z_hi, core).
Axes of the slice: x: 4, y: 8, z: 8 (z_hi: 4, z_lo: 2; z = z_hi * 2 + z_lo), core: 2. Of those that a mesh axis runs over, the one named last changes fastest.
Arguments:
- train_cells: bfloat16 [1024, 64, 192], P(('rows', 'feat')), may hold values from -7 to 7
- test_cells: bfloat16 [2048, 64, 192], P(('rows', 'feat')), may hold values from -7 to 7
- train_mask: int32 [1024, 64], P(('rows', 'feat')), may hold values from 0 to 1, as said below
- test_mask: int32 [2048, 64], P(('rows', 'feat')), may hold values 0 or 1
- feat_qkv: bfloat16 [192, 576], replicated, may hold values from -4 to 4
- feat_out: bfloat16 [192, 192], replicated, may hold values from -0.4375 to 0.4375
- feat_gain: float32 [192], replicated, may hold values from 0.5 to 1.5
- feat_bias: float32 [192], replicated, may hold values from -1 to 1
- item_qkv: bfloat16 [192, 576], replicated, may hold values from -4 to 4
- item_out: bfloat16 [192, 192], replicated, may hold values from -0.4375 to 0.4375
- item_gain: float32 [192], replicated, may hold values from 0.5 to 1.5
- item_bias: float32 [192], replicated, may hold values from -1 to 1
- mlp_in: bfloat16 [192, 768], replicated, may hold values from -0.4375 to 0.4375
- mlp_out: bfloat16 [768, 192], replicated, may hold values from -0.21875 to 0.21875
- mlp_gain: float32 [192], replicated, may hold values from 0.5 to 1.5
- mlp_bias: float32 [192], replicated, may hold values from -1 to 1
Outputs:
- train_out: bfloat16 [1024, 64, 192], P(('rows', 'feat'))
- test_out: bfloat16 [2048, 64, 192], P(('rows', 'feat'))
The draws below stay inside these ranges and needn't reach their ends.
Inputs may be any that keep to these rules, and one draw needn't show every extreme that they name: `train_mask`: each of the 64 features has at least one training row marked 1.
All inputs are finite; a program needn't handle non-finite values. No bound on the sum of `test_mask` on one device may be relied on, other than what follows from the above.
Results may differ from the reference program's by a relative error of at most 0.02.
The reference program's roundings to bfloat16 on the way count: a program that leaves them out, or rounds other values in their place, can miss the bound.
Values may be sent and summed in bfloat16 or wider, within the bound.
No kernel may reach another device: no remote copies, remote signals or barrier semaphores. Data moves between devices by JAX's collectives and lax.ppermute only.
A program may use at most 128 MiB of HBM per device.

```python
import math
import jax
import jax.numpy as jnp
from jax import lax

E = 192
HEADS = 6
FF = 768
F = 64
TRAIN = 1024
TEST = 2048


def table_pair(key):
    key_train = jax.random.fold_in(key, 7101)
    key_test = jax.random.fold_in(key, 7102)
    train_part = jax.random.normal(key_train, (TRAIN, F, E), jnp.float32)
    test_part = jax.random.normal(key_test, (TEST, F, E), jnp.float32)
    return (jnp.clip(train_part, -7.0, 7.0), jnp.clip(test_part, -7.0, 7.0))


def draw_train_cells(key, part):
    return table_pair(key)[0].astype(jnp.bfloat16)


def draw_test_cells(key, part):
    return table_pair(key)[1].astype(jnp.bfloat16)


def draw_train_mask(key, part):
    coarse = jax.random.randint(jax.random.fold_in(key, 7201), (TRAIN, F), 0, 4)
    chosen = jax.random.randint(jax.random.fold_in(key, 7202), (1, F), 0, TRAIN)
    forced = jnp.arange(TRAIN, dtype=jnp.int32)[:, None] == chosen
    return jnp.where(forced | (coarse > 0), 1, 0).astype(jnp.int32)


def attention_weight(key):
    query_part = 1.6 * jax.random.normal(jax.random.fold_in(key, 3), (E, E), jnp.float32) / math.sqrt(E)
    key_part = 1.6 * jax.random.normal(jax.random.fold_in(key, 4), (E, E), jnp.float32) / math.sqrt(E)
    value_part = jax.random.normal(jax.random.fold_in(key, 5), (E, E), jnp.float32) / math.sqrt(E)
    joined = jnp.concatenate([query_part, key_part, value_part], axis=1)
    return jnp.clip(joined, -4.0, 4.0).astype(jnp.bfloat16)


def draw_feat_qkv(key, part):
    return attention_weight(jax.random.fold_in(key, 7301))


def draw_item_qkv(key, part):
    return attention_weight(jax.random.fold_in(key, 7302))


def plant(entries, key, least, top_value):
    spot = [jax.random.randint(jax.random.fold_in(key, axis), (), 0, length) for axis, length in enumerate(entries.shape)]
    main_axis = entries.shape.index(max(entries.shape))
    next_to = spot[:main_axis] + [(spot[main_axis] + 1) % entries.shape[main_axis]] + spot[main_axis + 1:]
    return entries.at[tuple(spot)].set(least).at[tuple(next_to)].set(top_value)


def bell_draw(own_key, shape, width, limit, held_as=jnp.bfloat16):
    values = width * jax.random.normal(own_key, shape, jnp.float32)
    return jnp.clip(values, min=-limit, max=limit).astype(held_as)


def setup_inputs(seed: int = 0) -> dict:
    splits = jax.random.split(jax.random.key(seed), 17)
    return {
        "train_cells": draw_train_cells(jax.random.fold_in(splits[16], 71), 0),
        "test_cells": draw_test_cells(jax.random.fold_in(splits[16], 71), 0),
        "train_mask": draw_train_mask(jax.random.fold_in(splits[16], 71), 0),
        "test_mask": plant((jax.random.randint(splits[3], (TEST, F), 0, 4) < 3).astype(jnp.int32), jax.random.fold_in(splits[3], 1), 0, 1),
        "feat_qkv": draw_feat_qkv(jax.random.fold_in(splits[16], 71), 0),
        "feat_out": bell_draw(splits[5], (E, E), E ** -0.5, 0.4375),
        "feat_gain": jnp.clip(1.0 + 0.1 * jax.random.normal(splits[6], (E,), jnp.float32), 0.5, 1.5),
        "feat_bias": bell_draw(splits[7], (E,), 0.3, 1.0, jnp.float32),
        "item_qkv": draw_item_qkv(jax.random.fold_in(splits[16], 71), 0),
        "item_out": bell_draw(splits[9], (E, E), E ** -0.5, 0.4375),
        "item_gain": jnp.clip(1.0 + 0.1 * jax.random.normal(splits[10], (E,), jnp.float32), 0.5, 1.5),
        "item_bias": bell_draw(splits[11], (E,), 0.3, 1.0, jnp.float32),
        "mlp_in": bell_draw(splits[12], (E, FF), E ** -0.5, 0.4375),
        "mlp_out": bell_draw(splits[13], (FF, E), FF ** -0.5, 0.21875),
        "mlp_gain": jnp.clip(1.0 + 0.1 * jax.random.normal(splits[14], (E,), jnp.float32), 0.5, 1.5),
        "mlp_bias": bell_draw(splits[15], (E,), 0.3, 1.0, jnp.float32),
    }


EPS = 1e-05
NEG = -1e+30

def layer_norm(values, norm_gain, norm_bias):
    centre = lax.optimization_barrier(jnp.mean(values, axis=-1, keepdims=True))
    centred = values - centre
    variance = lax.optimization_barrier(jnp.mean(centred * centred, axis=-1, keepdims=True))
    return centred * lax.rsqrt(variance + EPS) * norm_gain + norm_bias

def feature_block(cell_rows, feat_qkv, feat_out, feat_gain, feat_bias):
    row_count = cell_rows.shape[0]
    head_size = E // HEADS
    flat_rows = cell_rows.reshape(row_count * F, E)
    packed = jnp.dot(flat_rows, feat_qkv, preferred_element_type=jnp.float32).astype(jnp.bfloat16)
    packed = lax.optimization_barrier(packed).astype(jnp.float32)
    packed = packed.reshape(row_count, F, 3, HEADS, head_size)
    scores = jnp.einsum('rqhd,rkhd->rhqk', packed[:, :, 0], packed[:, :, 1]) / math.sqrt(head_size)
    row_top = lax.optimization_barrier(jnp.max(scores, axis=-1, keepdims=True))
    weights_exp = jnp.exp(scores - row_top)
    weights = (weights_exp / lax.optimization_barrier(jnp.sum(weights_exp, axis=-1, keepdims=True))).astype(jnp.bfloat16)
    weights = lax.optimization_barrier(weights).astype(jnp.float32)
    attended = jnp.einsum('rhqk,rkhd->rqhd', weights, packed[:, :, 2]).astype(jnp.bfloat16)
    branch = jnp.dot(attended.reshape(row_count * F, E), feat_out, preferred_element_type=jnp.float32)
    settled = layer_norm(flat_rows.astype(jnp.float32) + branch, feat_gain, feat_bias)
    return settled.astype(jnp.bfloat16).reshape(row_count, F, E)

def feature_section(cell_rows, feat_qkv, feat_out, feat_gain, feat_bias):
    row_count = cell_rows.shape[0]
    block_rows = math.gcd(row_count, 256)
    blocks = cell_rows.reshape(row_count // block_rows, block_rows, F, E)
    settled = lax.map(lambda block_cells: feature_block(block_cells, feat_qkv, feat_out, feat_gain, feat_bias), blocks)
    return settled.reshape(row_count, F, E)

def item_column(query_cells, train_column, key_marks, item_qkv):
    query_count = query_cells.shape[0]
    head_size = E // HEADS
    queries = jnp.dot(query_cells, item_qkv[:, :E], preferred_element_type=jnp.float32).astype(jnp.bfloat16)
    queries = lax.optimization_barrier(queries).astype(jnp.float32).reshape(query_count, HEADS, head_size)
    key_values = jnp.dot(train_column, item_qkv[:, E:], preferred_element_type=jnp.float32).astype(jnp.bfloat16)
    key_values = lax.optimization_barrier(key_values).astype(jnp.float32).reshape(TRAIN, 2, HEADS, head_size)
    scores = jnp.einsum('qhd,khd->hqk', queries, key_values[:, 0]) / math.sqrt(head_size)
    alive_keys = (key_marks > 0)[None, None, :]
    masked = jnp.where(alive_keys, scores, NEG)
    row_top = lax.optimization_barrier(jnp.max(masked, axis=-1, keepdims=True))
    weights_exp = jnp.where(alive_keys, jnp.exp(masked - row_top), 0.0)
    totals = lax.optimization_barrier(jnp.sum(weights_exp, axis=-1))
    rounded = lax.optimization_barrier(weights_exp.astype(jnp.bfloat16)).astype(jnp.float32)
    weighted = jnp.einsum('hqk,khd->qhd', rounded, key_values[:, 1])
    attended = weighted / jnp.transpose(totals)[:, :, None]
    return attended.astype(jnp.bfloat16).reshape(query_count, E)

def reference(train_cells, test_cells, train_mask, test_mask, feat_qkv, feat_out, feat_gain, feat_bias, item_qkv, item_out, item_gain, item_bias, mlp_in, mlp_out, mlp_gain, mlp_bias):
    train_h = feature_section(train_cells, feat_qkv, feat_out, feat_gain, feat_bias)
    test_h = feature_section(test_cells, feat_qkv, feat_out, feat_gain, feat_bias)
    all_rows = jnp.concatenate([train_h, test_h], axis=0)
    query_count = all_rows.shape[0]
    columns = (jnp.swapaxes(all_rows, 0, 1), jnp.swapaxes(train_h, 0, 1), jnp.swapaxes(train_mask, 0, 1))
    attended = lax.map(lambda column_args: item_column(column_args[0], column_args[1], column_args[2], item_qkv), columns)
    attended = jnp.swapaxes(attended, 0, 1).reshape(query_count * F, E)
    branch = jnp.dot(attended, item_out, preferred_element_type=jnp.float32).reshape(query_count, F, E)
    keep_gate = jnp.concatenate([jnp.ones((TRAIN, F), jnp.float32), test_mask.astype(jnp.float32)], axis=0)
    branch = branch * keep_gate[:, :, None]
    settled = layer_norm(all_rows.astype(jnp.float32) + branch, item_gain, item_bias).astype(jnp.bfloat16)
    flat_rows = settled.reshape(query_count * F, E)
    hidden_units = jax.nn.gelu(jnp.dot(flat_rows, mlp_in, preferred_element_type=jnp.float32), approximate=False).astype(jnp.bfloat16)
    result_rows = layer_norm(flat_rows.astype(jnp.float32) + jnp.dot(hidden_units, mlp_out, preferred_element_type=jnp.float32), mlp_gain, mlp_bias)
    result_rows = result_rows.astype(jnp.bfloat16).reshape(query_count, F, E)
    return (result_rows[:TRAIN], result_rows[TRAIN:])
```

```python
import math

import jax
import jax.numpy as jnp
from jax import lax
from jax.sharding import PartitionSpec as P

HEADS = 6


EPS = 1e-05
NEG = -1e30


def layer_norm(values, norm_gain, norm_bias):
    centre = jnp.mean(values, axis=-1, keepdims=True)
    centred = values - centre
    variance = jnp.mean(centred * centred, axis=-1, keepdims=True)
    return centred * lax.rsqrt(variance + EPS) * norm_gain + norm_bias


def feature_block(cell_rows, qkv_weight, out_weight, norm_gain, norm_bias):
    row_count, feat_count, model_width = cell_rows.shape
    head_size = model_width // HEADS
    flat_rows = cell_rows.reshape(row_count * feat_count, model_width)
    packed = jnp.dot(flat_rows, qkv_weight, preferred_element_type=jnp.float32).astype(jnp.bfloat16)
    packed = packed.reshape(row_count, feat_count, 3, HEADS, head_size)
    scores = jnp.einsum(
        "rqhd,rkhd->rhqk", packed[:, :, 0], packed[:, :, 1], preferred_element_type=jnp.float32
    ) / math.sqrt(head_size)
    row_top = jnp.max(scores, axis=-1, keepdims=True)
    weights_exp = jnp.exp(scores - row_top)
    weights = (weights_exp / jnp.sum(weights_exp, axis=-1, keepdims=True)).astype(jnp.bfloat16)
    attended = jnp.einsum(
        "rhqk,rkhd->rqhd", weights, packed[:, :, 2], preferred_element_type=jnp.float32
    ).astype(jnp.bfloat16)
    branch = jnp.dot(
        attended.reshape(row_count * feat_count, model_width),
        out_weight,
        preferred_element_type=jnp.float32,
    )
    settled = layer_norm(flat_rows.astype(jnp.float32) + branch, norm_gain, norm_bias)
    return settled.astype(jnp.bfloat16).reshape(row_count, feat_count, model_width)


def item_attention(query_rows, key_rows, key_marks, item_qkv):
    query_count, model_width = query_rows.shape
    key_count = key_rows.shape[0]
    head_size = model_width // HEADS
    queries = jnp.dot(
        query_rows, item_qkv[:, :model_width], preferred_element_type=jnp.float32
    ).astype(jnp.bfloat16)
    queries = queries.reshape(query_count, HEADS, head_size)
    key_values = jnp.dot(
        key_rows, item_qkv[:, model_width:], preferred_element_type=jnp.float32
    ).astype(jnp.bfloat16)
    key_values = key_values.reshape(key_count, 2, HEADS, head_size)
    scores = jnp.einsum(
        "qhd,khd->hqk", queries, key_values[:, 0], preferred_element_type=jnp.float32
    ) / math.sqrt(head_size)
    alive_keys = (key_marks > 0)[None, None, :]
    masked = jnp.where(alive_keys, scores, NEG)
    row_top = jnp.max(masked, axis=-1, keepdims=True)
    weights_exp = jnp.where(alive_keys, jnp.exp(masked - row_top), 0.0)
    totals = jnp.sum(weights_exp, axis=-1)
    weighted = jnp.einsum(
        "hqk,khd->hqd",
        weights_exp.astype(jnp.bfloat16),
        key_values[:, 1],
        preferred_element_type=jnp.float32,
    )
    attended = (weighted / totals[..., None]).astype(jnp.bfloat16)
    return jnp.transpose(attended, (1, 0, 2)).reshape(query_count, model_width)


def per_device(
    train_cells,
    test_cells,
    train_mask,
    test_mask,
    feat_qkv,
    feat_out,
    feat_gain,
    feat_bias,
    item_qkv,
    item_out,
    item_gain,
    item_bias,
    mlp_in,
    mlp_out,
    mlp_gain,
    mlp_bias,
):
    train_count = train_cells.shape[0]
    row_count = train_count + test_cells.shape[0]
    feat_count, model_width = train_cells.shape[1], train_cells.shape[2]
    both_rows = jnp.concatenate([train_cells, test_cells], axis=0)
    settled = feature_block(both_rows, feat_qkv, feat_out, feat_gain, feat_bias)
    marks = jnp.concatenate([train_mask, test_mask], axis=0).astype(jnp.bfloat16)
    mark_row = jnp.pad(jnp.transpose(marks), ((0, 0), (0, model_width - row_count)))
    outbound = jnp.concatenate(
        [jnp.swapaxes(settled, 0, 1), mark_row[:, None, :]], axis=1
    )
    inbound = lax.all_to_all(outbound, "rows", split_axis=0, concat_axis=0, tiled=True)
    source_count = inbound.shape[0]
    col_rows = inbound[:, :row_count, :]
    col_marks = inbound[:, row_count, :row_count]
    train_rows = col_rows[:, :train_count].reshape(source_count * train_count, model_width)
    train_marks = col_marks[:, :train_count].reshape(source_count * train_count)
    local_keys = train_rows.shape[0]
    key_mark_row = jnp.pad(train_marks, (0, model_width - local_keys))
    gathered = lax.all_gather(
        jnp.concatenate([train_rows, key_mark_row[None, :]], axis=0), "feat", axis=0
    )
    key_rows = gathered[:, :local_keys].reshape(-1, model_width)
    key_marks = gathered[:, local_keys, :local_keys].reshape(-1)

    query_rows = col_rows.reshape(source_count * row_count, model_width)
    attended = item_attention(query_rows, key_rows, key_marks, item_qkv)
    branch = jnp.dot(attended, item_out, preferred_element_type=jnp.float32)
    is_train = (jnp.arange(row_count) < train_count)[None, :]
    keep_gate = jnp.where(is_train, jnp.ones_like(col_marks), col_marks).astype(jnp.float32)
    branch = branch * keep_gate.reshape(-1, 1)
    settled_item = layer_norm(
        query_rows.astype(jnp.float32) + branch, item_gain, item_bias
    ).astype(jnp.bfloat16)
    hidden_units = jax.nn.gelu(
        jnp.dot(settled_item, mlp_in, preferred_element_type=jnp.float32), approximate=False
    ).astype(jnp.bfloat16)
    result_rows = layer_norm(
        settled_item.astype(jnp.float32)
        + jnp.dot(hidden_units, mlp_out, preferred_element_type=jnp.float32),
        mlp_gain,
        mlp_bias,
    ).astype(jnp.bfloat16)
    result_rows = result_rows.reshape(source_count, row_count, model_width)
    returned = lax.all_to_all(result_rows, "rows", split_axis=0, concat_axis=0, tiled=True)
    final = jnp.swapaxes(returned, 0, 1)
    return (final[:train_count], final[train_count:])


def solution(mesh):
    return jax.shard_map(
        per_device,
        mesh=mesh,
        in_specs=(
            P(("rows", "feat"), None, None),
            P(("rows", "feat"), None, None),
            P(("rows", "feat"), None),
            P(("rows", "feat"), None),
            P(),
            P(),
            P(),
            P(),
            P(),
            P(),
            P(),
            P(),
            P(),
            P(),
            P(),
            P(),
        ),
        out_specs=(P(("rows", "feat"), None, None), P(("rows", "feat"), None, None)),
        check_vma=False,
    )
```

```python
import math

import jax
import jax.numpy as jnp
from jax import lax
from jax.experimental import pallas as pl
from jax.sharding import PartitionSpec as P

HEADS = 6


EPS = 1e-05
NEG = -1e30


def layer_norm(values, norm_gain, norm_bias):
    centre = jnp.mean(values, axis=-1, keepdims=True)
    centred = values - centre
    variance = jnp.mean(centred * centred, axis=-1, keepdims=True)
    return centred * lax.rsqrt(variance + EPS) * norm_gain + norm_bias


def feature_block(cell_rows, qkv_weight, out_weight, norm_gain, norm_bias):
    row_count, feat_count, model_width = cell_rows.shape
    head_size = model_width // HEADS
    flat_rows = cell_rows.reshape(row_count * feat_count, model_width)
    packed = jnp.dot(flat_rows, qkv_weight, preferred_element_type=jnp.float32).astype(jnp.bfloat16)
    packed = packed.reshape(row_count, feat_count, 3, HEADS, head_size)
    scores = jnp.einsum(
        "rqhd,rkhd->rhqk", packed[:, :, 0], packed[:, :, 1], preferred_element_type=jnp.float32
    ) / math.sqrt(head_size)
    row_top = jnp.max(scores, axis=-1, keepdims=True)
    weights_exp = jnp.exp(scores - row_top)
    weights = (weights_exp / jnp.sum(weights_exp, axis=-1, keepdims=True)).astype(jnp.bfloat16)
    attended = jnp.einsum(
        "rhqk,rkhd->rqhd", weights, packed[:, :, 2], preferred_element_type=jnp.float32
    ).astype(jnp.bfloat16)
    branch = jnp.dot(
        attended.reshape(row_count * feat_count, model_width),
        out_weight,
        preferred_element_type=jnp.float32,
    )
    settled = layer_norm(flat_rows.astype(jnp.float32) + branch, norm_gain, norm_bias)
    return settled.astype(jnp.bfloat16).reshape(row_count, feat_count, model_width)


def attention_kernel(query_ref, key_ref, value_ref, mark_ref, out_ref):
    head_size = query_ref.shape[-1]
    scores = lax.dot_general(
        query_ref[0], key_ref[0], (((1,), (1,)), ((), ())), preferred_element_type=jnp.float32
    ) / math.sqrt(head_size)
    alive_keys = mark_ref[...] > 0
    masked = jnp.where(alive_keys, scores, NEG)
    row_top = jnp.max(masked, axis=-1, keepdims=True)
    weights_exp = jnp.where(alive_keys, jnp.exp(masked - row_top), 0.0)
    totals = jnp.sum(weights_exp, axis=-1, keepdims=True)
    weighted = jnp.dot(
        weights_exp.astype(jnp.bfloat16), value_ref[0], preferred_element_type=jnp.float32
    )
    out_ref[0] = (weighted / totals).astype(out_ref.dtype)


def item_attention(query_rows, key_rows, key_marks, item_qkv):
    query_count, model_width = query_rows.shape
    key_count = key_rows.shape[0]
    head_size = model_width // HEADS
    queries = jnp.dot(
        query_rows, item_qkv[:, :model_width], preferred_element_type=jnp.float32
    ).astype(jnp.bfloat16)
    queries = jnp.transpose(queries.reshape(query_count, HEADS, head_size), (1, 0, 2))
    key_values = jnp.dot(
        key_rows, item_qkv[:, model_width:], preferred_element_type=jnp.float32
    ).astype(jnp.bfloat16)
    key_values = jnp.transpose(key_values.reshape(key_count, 2 * HEADS, head_size), (1, 0, 2))
    marks = key_marks.astype(jnp.float32).reshape(1, key_count)
    attended = pl.pallas_call(
        attention_kernel,
        grid=(HEADS,),
        in_specs=[
            pl.BlockSpec((1, query_count, head_size), lambda h: (h, 0, 0)),
            pl.BlockSpec((1, key_count, head_size), lambda h: (h, 0, 0)),
            pl.BlockSpec((1, key_count, head_size), lambda h: (h + HEADS, 0, 0)),
            pl.BlockSpec((1, key_count), lambda h: (0, 0)),
        ],
        out_specs=pl.BlockSpec((1, query_count, head_size), lambda h: (h, 0, 0)),
        out_shape=jax.ShapeDtypeStruct((HEADS, query_count, head_size), jnp.bfloat16),
        cost_estimate=pl.CostEstimate(
            flops=4 * HEADS * query_count * key_count * head_size,
            transcendentals=HEADS * query_count * key_count,
            bytes_accessed=2 * (2 * query_count + 2 * key_count) * model_width,
        ),
    )(queries, key_values, key_values, marks)
    return jnp.transpose(attended, (1, 0, 2)).reshape(query_count, model_width)


def per_device(
    train_cells,
    test_cells,
    train_mask,
    test_mask,
    feat_qkv,
    feat_out,
    feat_gain,
    feat_bias,
    item_qkv,
    item_out,
    item_gain,
    item_bias,
    mlp_in,
    mlp_out,
    mlp_gain,
    mlp_bias,
):
    train_count = train_cells.shape[0]
    row_count = train_count + test_cells.shape[0]
    feat_count, model_width = train_cells.shape[1], train_cells.shape[2]
    both_rows = jnp.concatenate([train_cells, test_cells], axis=0)
    settled = feature_block(both_rows, feat_qkv, feat_out, feat_gain, feat_bias)
    marks = jnp.concatenate([train_mask, test_mask], axis=0).astype(jnp.bfloat16)
    mark_row = jnp.pad(jnp.transpose(marks), ((0, 0), (0, model_width - row_count)))
    outbound = jnp.concatenate(
        [jnp.swapaxes(settled, 0, 1), mark_row[:, None, :]], axis=1
    )
    inbound = lax.all_to_all(outbound, "rows", split_axis=0, concat_axis=0, tiled=True)
    source_count = inbound.shape[0]
    col_rows = inbound[:, :row_count, :]
    col_marks = inbound[:, row_count, :row_count]
    train_rows = col_rows[:, :train_count].reshape(source_count * train_count, model_width)
    train_marks = col_marks[:, :train_count].reshape(source_count * train_count)
    local_keys = train_rows.shape[0]
    key_mark_row = jnp.pad(train_marks, (0, model_width - local_keys))
    gathered = lax.all_gather(
        jnp.concatenate([train_rows, key_mark_row[None, :]], axis=0), "feat", axis=0
    )
    key_rows = gathered[:, :local_keys].reshape(-1, model_width)
    key_marks = gathered[:, local_keys, :local_keys].reshape(-1)

    query_rows = col_rows.reshape(source_count * row_count, model_width)
    attended = item_attention(query_rows, key_rows, key_marks, item_qkv)
    branch = jnp.dot(attended, item_out, preferred_element_type=jnp.float32)
    is_train = (jnp.arange(row_count) < train_count)[None, :]
    keep_gate = jnp.where(is_train, jnp.ones_like(col_marks), col_marks).astype(jnp.float32)
    branch = branch * keep_gate.reshape(-1, 1)
    settled_item = layer_norm(
        query_rows.astype(jnp.float32) + branch, item_gain, item_bias
    ).astype(jnp.bfloat16)
    hidden_units = jax.nn.gelu(
        jnp.dot(settled_item, mlp_in, preferred_element_type=jnp.float32), approximate=False
    ).astype(jnp.bfloat16)
    result_rows = layer_norm(
        settled_item.astype(jnp.float32)
        + jnp.dot(hidden_units, mlp_out, preferred_element_type=jnp.float32),
        mlp_gain,
        mlp_bias,
    ).astype(jnp.bfloat16)
    result_rows = result_rows.reshape(source_count, row_count, model_width)
    returned = lax.all_to_all(result_rows, "rows", split_axis=0, concat_axis=0, tiled=True)
    final = jnp.swapaxes(returned, 0, 1)
    return (final[:train_count], final[train_count:])


def solution(mesh):
    return jax.shard_map(
        per_device,
        mesh=mesh,
        in_specs=(
            P(("rows", "feat"), None, None),
            P(("rows", "feat"), None, None),
            P(("rows", "feat"), None),
            P(("rows", "feat"), None),
            P(),
            P(),
            P(),
            P(),
            P(),
            P(),
            P(),
            P(),
            P(),
            P(),
            P(),
            P(),
        ),
        out_specs=(P(("rows", "feat"), None, None), P(("rows", "feat"), None, None)),
        check_vma=False,
    )
```

```python
import math

import jax
import jax.numpy as jnp
from jax import lax
from jax.experimental import pallas as pl
from jax.sharding import PartitionSpec as P

HEADS = 6


EPS = 1e-05
NEG = -1e30


def layer_norm(values, norm_gain, norm_bias):
    centre = jnp.mean(values, axis=-1, keepdims=True)
    centred = values - centre
    variance = jnp.mean(centred * centred, axis=-1, keepdims=True)
    return centred * lax.rsqrt(variance + EPS) * norm_gain + norm_bias


def feature_block(cell_rows, qkv_weight, out_weight, norm_gain, norm_bias):
    row_count, feat_count, model_width = cell_rows.shape
    head_size = model_width // HEADS
    flat_rows = cell_rows.reshape(row_count * feat_count, model_width)
    packed = jnp.dot(flat_rows, qkv_weight, preferred_element_type=jnp.float32).astype(jnp.bfloat16)
    packed = packed.reshape(row_count, feat_count, 3, HEADS, head_size)
    scores = jnp.einsum(
        "rqhd,rkhd->rhqk", packed[:, :, 0], packed[:, :, 1], preferred_element_type=jnp.float32
    ) / math.sqrt(head_size)
    row_top = jnp.max(scores, axis=-1, keepdims=True)
    weights_exp = jnp.exp(scores - row_top)
    weights = (weights_exp / jnp.sum(weights_exp, axis=-1, keepdims=True)).astype(jnp.bfloat16)
    attended = jnp.einsum(
        "rhqk,rkhd->rqhd", weights, packed[:, :, 2], preferred_element_type=jnp.float32
    ).astype(jnp.bfloat16)
    branch = jnp.dot(
        attended.reshape(row_count * feat_count, model_width),
        out_weight,
        preferred_element_type=jnp.float32,
    )
    settled = layer_norm(flat_rows.astype(jnp.float32) + branch, norm_gain, norm_bias)
    return settled.astype(jnp.bfloat16).reshape(row_count, feat_count, model_width)


def attention_kernel(query_ref, key_ref, value_ref, mark_ref, out_ref):
    head_size = query_ref.shape[0]
    scores = lax.dot_general(
        key_ref[...], query_ref[...], (((0,), (0,)), ((), ())), preferred_element_type=jnp.float32
    ) / math.sqrt(head_size)
    masked = jnp.where(mark_ref[...] > 0, scores, NEG)
    row_top = jnp.max(masked, axis=0, keepdims=True)
    weights_exp = jnp.exp(masked - row_top)
    totals = jnp.sum(weights_exp, axis=0, keepdims=True)
    weighted = jnp.dot(
        value_ref[...], weights_exp.astype(jnp.bfloat16), preferred_element_type=jnp.float32
    )
    out_ref[...] = (weighted / totals).astype(out_ref.dtype)


def item_attention(query_rows, key_rows, key_marks, item_qkv):
    query_count, model_width = query_rows.shape
    key_count = key_rows.shape[0]
    head_size = model_width // HEADS
    queries_t = lax.dot_general(
        item_qkv[:, :model_width], query_rows, (((0,), (1,)), ((), ())),
        preferred_element_type=jnp.float32,
    ).astype(jnp.bfloat16)
    key_values_t = lax.dot_general(
        item_qkv[:, model_width:], key_rows, (((0,), (1,)), ((), ())),
        preferred_element_type=jnp.float32,
    ).astype(jnp.bfloat16)
    marks = key_marks.astype(jnp.float32).reshape(key_count, 1)
    attended_t = pl.pallas_call(
        attention_kernel,
        grid=(HEADS,),
        in_specs=[
            pl.BlockSpec((head_size, query_count), lambda h: (h, 0)),
            pl.BlockSpec((head_size, key_count), lambda h: (h, 0)),
            pl.BlockSpec((head_size, key_count), lambda h: (h + HEADS, 0)),
            pl.BlockSpec((key_count, 1), lambda h: (0, 0)),
        ],
        out_specs=pl.BlockSpec((head_size, query_count), lambda h: (h, 0)),
        out_shape=jax.ShapeDtypeStruct((model_width, query_count), jnp.bfloat16),
        cost_estimate=pl.CostEstimate(
            flops=4 * HEADS * query_count * key_count * head_size,
            transcendentals=HEADS * query_count * key_count,
            bytes_accessed=2 * (2 * query_count + 2 * key_count) * model_width,
        ),
    )(queries_t, key_values_t, key_values_t, marks)
    return attended_t


def per_device(
    train_cells,
    test_cells,
    train_mask,
    test_mask,
    feat_qkv,
    feat_out,
    feat_gain,
    feat_bias,
    item_qkv,
    item_out,
    item_gain,
    item_bias,
    mlp_in,
    mlp_out,
    mlp_gain,
    mlp_bias,
):
    train_count = train_cells.shape[0]
    row_count = train_count + test_cells.shape[0]
    feat_count, model_width = train_cells.shape[1], train_cells.shape[2]
    both_rows = jnp.concatenate([train_cells, test_cells], axis=0)
    settled = feature_block(both_rows, feat_qkv, feat_out, feat_gain, feat_bias)
    marks = jnp.concatenate([train_mask, test_mask], axis=0).astype(jnp.bfloat16)
    mark_row = jnp.pad(jnp.transpose(marks), ((0, 0), (0, model_width - row_count)))
    outbound = jnp.concatenate(
        [jnp.swapaxes(settled, 0, 1), mark_row[:, None, :]], axis=1
    )
    inbound = lax.all_to_all(outbound, "rows", split_axis=0, concat_axis=0, tiled=True)
    source_count = inbound.shape[0]
    col_rows = inbound[:, :row_count, :]
    col_marks = inbound[:, row_count, :row_count]
    train_rows = col_rows[:, :train_count].reshape(source_count * train_count, model_width)
    train_marks = col_marks[:, :train_count].reshape(source_count * train_count)
    local_keys = train_rows.shape[0]
    key_mark_row = jnp.pad(train_marks, (0, model_width - local_keys))
    gathered = lax.all_gather(
        jnp.concatenate([train_rows, key_mark_row[None, :]], axis=0), "feat", axis=0
    )
    key_rows = gathered[:, :local_keys].reshape(-1, model_width)
    key_marks = gathered[:, local_keys, :local_keys].reshape(-1)

    query_rows = col_rows.reshape(source_count * row_count, model_width)
    attended_t = item_attention(query_rows, key_rows, key_marks, item_qkv)
    branch = lax.dot_general(
        attended_t, item_out, (((0,), (0,)), ((), ())), preferred_element_type=jnp.float32
    )
    is_train = (jnp.arange(row_count) < train_count)[None, :]
    keep_gate = jnp.where(is_train, jnp.ones_like(col_marks), col_marks).astype(jnp.float32)
    branch = branch * keep_gate.reshape(-1, 1)
    settled_item = layer_norm(
        query_rows.astype(jnp.float32) + branch, item_gain, item_bias
    ).astype(jnp.bfloat16)
    hidden_units = jax.nn.gelu(
        jnp.dot(settled_item, mlp_in, preferred_element_type=jnp.float32), approximate=False
    ).astype(jnp.bfloat16)
    result_rows = layer_norm(
        settled_item.astype(jnp.float32)
        + jnp.dot(hidden_units, mlp_out, preferred_element_type=jnp.float32),
        mlp_gain,
        mlp_bias,
    ).astype(jnp.bfloat16)
    result_rows = result_rows.reshape(source_count, row_count, model_width)
    returned = lax.all_to_all(result_rows, "rows", split_axis=0, concat_axis=0, tiled=True)
    final = jnp.swapaxes(returned, 0, 1)
    return (final[:train_count], final[train_count:])


def solution(mesh):
    return jax.shard_map(
        per_device,
        mesh=mesh,
        in_specs=(
            P(("rows", "feat"), None, None),
            P(("rows", "feat"), None, None),
            P(("rows", "feat"), None),
            P(("rows", "feat"), None),
            P(),
            P(),
            P(),
            P(),
            P(),
            P(),
            P(),
            P(),
            P(),
            P(),
            P(),
            P(),
        ),
        out_specs=(P(("rows", "feat"), None, None), P(("rows", "feat"), None, None)),
        check_vma=False,
    )
```

```python
import math

import jax
import jax.numpy as jnp
from jax import lax
from jax.sharding import PartitionSpec as P

HEADS = 6


EPS = 1e-05
NEG = -1e30


def layer_norm(values, norm_gain, norm_bias):
    centre = jnp.mean(values, axis=-1, keepdims=True)
    centred = values - centre
    variance = jnp.mean(centred * centred, axis=-1, keepdims=True)
    return centred * lax.rsqrt(variance + EPS) * norm_gain + norm_bias


def feature_block(cell_rows, qkv_weight, out_weight, norm_gain, norm_bias):
    row_count, feat_count, model_width = cell_rows.shape
    head_size = model_width // HEADS
    flat_rows = cell_rows.reshape(row_count * feat_count, model_width)
    head_weights = qkv_weight.reshape(model_width, 3, HEADS, head_size)
    packed = jnp.einsum(
        "rfc,cthd->trhfd", cell_rows, head_weights, preferred_element_type=jnp.float32
    ).astype(jnp.bfloat16)
    scores = jnp.einsum(
        "rhqd,rhkd->rhqk", packed[0], packed[1], preferred_element_type=jnp.float32
    ) / math.sqrt(head_size)
    row_top = jnp.max(scores, axis=-1, keepdims=True)
    weights_exp = jnp.exp(scores - row_top)
    weights = (weights_exp / jnp.sum(weights_exp, axis=-1, keepdims=True)).astype(jnp.bfloat16)
    attended = jnp.einsum(
        "rhqk,rhkd->rhqd", weights, packed[2], preferred_element_type=jnp.float32
    ).astype(jnp.bfloat16)
    branch = jnp.einsum(
        "rhqd,hde->rqe",
        attended,
        out_weight.reshape(HEADS, head_size, model_width),
        preferred_element_type=jnp.float32,
    ).reshape(row_count * feat_count, model_width)
    settled = layer_norm(flat_rows.astype(jnp.float32) + branch, norm_gain, norm_bias)
    return settled.astype(jnp.bfloat16).reshape(row_count, feat_count, model_width)


def item_attention(query_rows, key_rows, key_marks, item_qkv, item_out):
    model_width = query_rows.shape[1]
    head_size = model_width // HEADS
    query_weights = item_qkv[:, :model_width].reshape(model_width, HEADS, head_size)
    pair_weights = item_qkv[:, model_width:].reshape(model_width, 2, HEADS, head_size)
    queries = jnp.einsum(
        "nc,chd->hnd", query_rows, query_weights, preferred_element_type=jnp.float32
    ).astype(jnp.bfloat16)
    key_values = jnp.einsum(
        "kc,cthd->thkd", key_rows, pair_weights, preferred_element_type=jnp.float32
    ).astype(jnp.bfloat16)
    scores = jnp.einsum(
        "hnd,hkd->hnk", queries, key_values[0], preferred_element_type=jnp.float32
    ) / math.sqrt(head_size)
    masked = jnp.where((key_marks > 0)[None, None, :], scores, NEG)
    row_top = jnp.max(masked, axis=-1, keepdims=True)
    weights_exp = jnp.exp(masked - row_top)
    totals = jnp.sum(weights_exp, axis=-1)
    weighted = jnp.einsum(
        "hnk,hkd->hnd",
        weights_exp.astype(jnp.bfloat16),
        key_values[1],
        preferred_element_type=jnp.float32,
    )
    attended = (weighted / totals[..., None]).astype(jnp.bfloat16)
    return jnp.einsum(
        "hnd,hde->ne",
        attended,
        item_out.reshape(HEADS, head_size, model_width),
        preferred_element_type=jnp.float32,
    )


def per_device(
    train_cells,
    test_cells,
    train_mask,
    test_mask,
    feat_qkv,
    feat_out,
    feat_gain,
    feat_bias,
    item_qkv,
    item_out,
    item_gain,
    item_bias,
    mlp_in,
    mlp_out,
    mlp_gain,
    mlp_bias,
):
    train_count = train_cells.shape[0]
    row_count = train_count + test_cells.shape[0]
    feat_count, model_width = train_cells.shape[1], train_cells.shape[2]
    both_rows = jnp.concatenate([train_cells, test_cells], axis=0)
    settled = feature_block(both_rows, feat_qkv, feat_out, feat_gain, feat_bias)
    marks = jnp.concatenate([train_mask, test_mask], axis=0).astype(jnp.bfloat16)
    mark_row = jnp.pad(jnp.transpose(marks), ((0, 0), (0, model_width - row_count)))
    outbound = jnp.concatenate(
        [jnp.swapaxes(settled, 0, 1), mark_row[:, None, :]], axis=1
    )
    inbound = lax.all_to_all(outbound, "rows", split_axis=0, concat_axis=0, tiled=True)
    source_count = inbound.shape[0]
    col_rows = inbound[:, :row_count, :]
    col_marks = inbound[:, row_count, :row_count]
    train_rows = col_rows[:, :train_count].reshape(source_count * train_count, model_width)
    train_marks = col_marks[:, :train_count].reshape(source_count * train_count)
    local_keys = train_rows.shape[0]
    key_mark_row = jnp.pad(train_marks, (0, model_width - local_keys))
    gathered = lax.all_gather(
        jnp.concatenate([train_rows, key_mark_row[None, :]], axis=0), "feat", axis=0
    )
    key_rows = gathered[:, :local_keys].reshape(-1, model_width)
    key_marks = gathered[:, local_keys, :local_keys].reshape(-1)

    query_rows = col_rows.reshape(source_count * row_count, model_width)
    branch = item_attention(query_rows, key_rows, key_marks, item_qkv, item_out)
    is_train = (jnp.arange(row_count) < train_count)[None, :]
    keep_gate = jnp.where(is_train, jnp.ones_like(col_marks), col_marks).astype(jnp.float32)
    branch = branch * keep_gate.reshape(-1, 1)
    settled_item = layer_norm(
        query_rows.astype(jnp.float32) + branch, item_gain, item_bias
    ).astype(jnp.bfloat16)
    hidden_units = jax.nn.gelu(
        jnp.dot(settled_item, mlp_in, preferred_element_type=jnp.float32), approximate=False
    ).astype(jnp.bfloat16)
    result_rows = layer_norm(
        settled_item.astype(jnp.float32)
        + jnp.dot(hidden_units, mlp_out, preferred_element_type=jnp.float32),
        mlp_gain,
        mlp_bias,
    ).astype(jnp.bfloat16)
    result_rows = result_rows.reshape(source_count, row_count, model_width)
    returned = lax.all_to_all(result_rows, "rows", split_axis=0, concat_axis=0, tiled=True)
    final = jnp.swapaxes(returned, 0, 1)
    return (final[:train_count], final[train_count:])


def solution(mesh):
    return jax.shard_map(
        per_device,
        mesh=mesh,
        in_specs=(
            P(("rows", "feat"), None, None),
            P(("rows", "feat"), None, None),
            P(("rows", "feat"), None),
            P(("rows", "feat"), None),
            P(),
            P(),
            P(),
            P(),
            P(),
            P(),
            P(),
            P(),
            P(),
            P(),
            P(),
            P(),
        ),
        out_specs=(P(("rows", "feat"), None, None), P(("rows", "feat"), None, None)),
        check_vma=False,
    )
```

```python
import functools
import math

import jax
import jax.numpy as jnp
from jax import lax
from jax.experimental import pallas as pl
from jax.sharding import PartitionSpec as P

HEADS = 6


EPS = 1e-05
NEG = -1e30


def layer_norm(values, norm_gain, norm_bias):
    centre = jnp.mean(values, axis=-1, keepdims=True)
    centred = values - centre
    variance = jnp.mean(centred * centred, axis=-1, keepdims=True)
    return centred * lax.rsqrt(variance + EPS) * norm_gain + norm_bias


def feature_kernel(
    feat_count,
    cells_ref, query_w_ref, key_w_ref, value_w_ref, out_w_ref, gain_ref, bias_ref, settled_ref
):
    cell_count, model_width = cells_ref.shape
    head_size = model_width // HEADS
    row_count = cell_count // feat_count
    cells = cells_ref[...]
    branch = jnp.zeros((cell_count, model_width), jnp.float32)
    for head in range(HEADS):
        queries = jnp.dot(cells, query_w_ref[head], preferred_element_type=jnp.float32).astype(jnp.bfloat16)
        keys = jnp.dot(cells, key_w_ref[head], preferred_element_type=jnp.float32).astype(jnp.bfloat16)
        values = jnp.dot(cells, value_w_ref[head], preferred_element_type=jnp.float32).astype(jnp.bfloat16)
        mixed_rows = []
        for row in range(row_count):
            part = slice(row * feat_count, (row + 1) * feat_count)
            scores = lax.dot_general(
                queries[part], keys[part], (((1,), (1,)), ((), ())),
                preferred_element_type=jnp.float32,
            ) / math.sqrt(head_size)
            row_top = jnp.max(scores, axis=-1, keepdims=True)
            weights_exp = jnp.exp(scores - row_top)
            weights = (weights_exp / jnp.sum(weights_exp, axis=-1, keepdims=True)).astype(jnp.bfloat16)
            mixed_rows.append(
                jnp.dot(weights, values[part], preferred_element_type=jnp.float32).astype(jnp.bfloat16)
            )
        mixed = jnp.concatenate(mixed_rows, axis=0)
        branch = branch + jnp.dot(mixed, out_w_ref[head], preferred_element_type=jnp.float32)
    values_sum = cells.astype(jnp.float32) + branch
    centre = jnp.mean(values_sum, axis=-1, keepdims=True)
    centred = values_sum - centre
    variance = jnp.mean(centred * centred, axis=-1, keepdims=True)
    settled = centred * lax.rsqrt(variance + EPS) * gain_ref[...] + bias_ref[...]
    settled_ref[...] = settled.astype(settled_ref.dtype)


def feature_block(cell_rows, qkv_weight, out_weight, norm_gain, norm_bias):
    row_count, feat_count, model_width = cell_rows.shape
    head_size = model_width // HEADS
    flat_rows = cell_rows.reshape(row_count * feat_count, model_width)
    head_weights = jnp.transpose(
        qkv_weight.reshape(model_width, 3, HEADS, head_size), (1, 2, 0, 3)
    )
    whole = lambda shape: pl.BlockSpec(shape, lambda: (0,) * len(shape))
    settled = pl.pallas_call(
        functools.partial(feature_kernel, feat_count),
        in_specs=[
            whole((row_count * feat_count, model_width)),
            whole((HEADS, model_width, head_size)),
            whole((HEADS, model_width, head_size)),
            whole((HEADS, model_width, head_size)),
            whole((HEADS, head_size, model_width)),
            whole((1, model_width)),
            whole((1, model_width)),
        ],
        out_specs=whole((row_count * feat_count, model_width)),
        out_shape=jax.ShapeDtypeStruct((row_count * feat_count, model_width), jnp.bfloat16),
        cost_estimate=pl.CostEstimate(
            flops=2 * row_count * feat_count * model_width * (4 * model_width + 2 * feat_count),
            transcendentals=row_count * HEADS * feat_count * feat_count,
            bytes_accessed=4 * row_count * feat_count * model_width,
        ),
    )(
        flat_rows,
        head_weights[0],
        head_weights[1],
        head_weights[2],
        out_weight.reshape(HEADS, head_size, model_width),
        norm_gain.reshape(1, model_width),
        norm_bias.reshape(1, model_width),
    )
    return settled.reshape(row_count, feat_count, model_width)


def item_attention(query_rows, key_rows, key_marks, item_qkv):
    query_count, model_width = query_rows.shape
    key_count = key_rows.shape[0]
    head_size = model_width // HEADS
    queries = jnp.dot(
        query_rows, item_qkv[:, :model_width], preferred_element_type=jnp.float32
    ).astype(jnp.bfloat16)
    queries = queries.reshape(query_count, HEADS, head_size)
    key_values = jnp.dot(
        key_rows, item_qkv[:, model_width:], preferred_element_type=jnp.float32
    ).astype(jnp.bfloat16)
    key_values = key_values.reshape(key_count, 2, HEADS, head_size)
    scores = jnp.einsum(
        "qhd,khd->hqk", queries, key_values[:, 0], preferred_element_type=jnp.float32
    ) / math.sqrt(head_size)
    alive_keys = (key_marks > 0)[None, None, :]
    masked = jnp.where(alive_keys, scores, NEG)
    row_top = jnp.max(masked, axis=-1, keepdims=True)
    weights_exp = jnp.where(alive_keys, jnp.exp(masked - row_top), 0.0)
    totals = jnp.sum(weights_exp, axis=-1)
    weighted = jnp.einsum(
        "hqk,khd->hqd",
        weights_exp.astype(jnp.bfloat16),
        key_values[:, 1],
        preferred_element_type=jnp.float32,
    )
    attended = (weighted / totals[..., None]).astype(jnp.bfloat16)
    return jnp.transpose(attended, (1, 0, 2)).reshape(query_count, model_width)


def per_device(
    train_cells,
    test_cells,
    train_mask,
    test_mask,
    feat_qkv,
    feat_out,
    feat_gain,
    feat_bias,
    item_qkv,
    item_out,
    item_gain,
    item_bias,
    mlp_in,
    mlp_out,
    mlp_gain,
    mlp_bias,
):
    train_count = train_cells.shape[0]
    row_count = train_count + test_cells.shape[0]
    feat_count, model_width = train_cells.shape[1], train_cells.shape[2]
    both_rows = jnp.concatenate([train_cells, test_cells], axis=0)
    settled = feature_block(both_rows, feat_qkv, feat_out, feat_gain, feat_bias)
    marks = jnp.concatenate([train_mask, test_mask], axis=0).astype(jnp.bfloat16)
    mark_row = jnp.pad(jnp.transpose(marks), ((0, 0), (0, model_width - row_count)))
    outbound = jnp.concatenate(
        [jnp.swapaxes(settled, 0, 1), mark_row[:, None, :]], axis=1
    )
    inbound = lax.all_to_all(outbound, "rows", split_axis=0, concat_axis=0, tiled=True)
    source_count = inbound.shape[0]
    col_rows = inbound[:, :row_count, :]
    col_marks = inbound[:, row_count, :row_count]
    train_rows = col_rows[:, :train_count].reshape(source_count * train_count, model_width)
    train_marks = col_marks[:, :train_count].reshape(source_count * train_count)
    local_keys = train_rows.shape[0]
    key_mark_row = jnp.pad(train_marks, (0, model_width - local_keys))
    gathered = lax.all_gather(
        jnp.concatenate([train_rows, key_mark_row[None, :]], axis=0), "feat", axis=0
    )
    key_rows = gathered[:, :local_keys].reshape(-1, model_width)
    key_marks = gathered[:, local_keys, :local_keys].reshape(-1)

    query_rows = col_rows.reshape(source_count * row_count, model_width)
    attended = item_attention(query_rows, key_rows, key_marks, item_qkv)
    branch = jnp.dot(attended, item_out, preferred_element_type=jnp.float32)
    is_train = (jnp.arange(row_count) < train_count)[None, :]
    keep_gate = jnp.where(is_train, jnp.ones_like(col_marks), col_marks).astype(jnp.float32)
    branch = branch * keep_gate.reshape(-1, 1)
    settled_item = layer_norm(
        query_rows.astype(jnp.float32) + branch, item_gain, item_bias
    ).astype(jnp.bfloat16)
    hidden_units = jax.nn.gelu(
        jnp.dot(settled_item, mlp_in, preferred_element_type=jnp.float32), approximate=False
    ).astype(jnp.bfloat16)
    result_rows = layer_norm(
        settled_item.astype(jnp.float32)
        + jnp.dot(hidden_units, mlp_out, preferred_element_type=jnp.float32),
        mlp_gain,
        mlp_bias,
    ).astype(jnp.bfloat16)
    result_rows = result_rows.reshape(source_count, row_count, model_width)
    returned = lax.all_to_all(result_rows, "rows", split_axis=0, concat_axis=0, tiled=True)
    final = jnp.swapaxes(returned, 0, 1)
    return (final[:train_count], final[train_count:])


def solution(mesh):
    return jax.shard_map(
        per_device,
        mesh=mesh,
        in_specs=(
            P(("rows", "feat"), None, None),
            P(("rows", "feat"), None, None),
            P(("rows", "feat"), None),
            P(("rows", "feat"), None),
            P(),
            P(),
            P(),
            P(),
            P(),
            P(),
            P(),
            P(),
            P(),
            P(),
            P(),
            P(),
        ),
        out_specs=(P(("rows", "feat"), None, None), P(("rows", "feat"), None, None)),
        check_vma=False,
    )
```

```python
import math

import jax
import jax.numpy as jnp
from jax import lax
from jax.sharding import PartitionSpec as P

HEADS = 6


EPS = 1e-05
NEG = -1e30


def layer_norm(values, norm_gain, norm_bias):
    centre = jnp.mean(values, axis=-1, keepdims=True)
    centred = values - centre
    variance = jnp.mean(centred * centred, axis=-1, keepdims=True)
    return centred * lax.rsqrt(variance + EPS) * norm_gain + norm_bias


def feature_block(cell_rows, qkv_weight, out_weight, norm_gain, norm_bias):
    row_count, feat_count, model_width = cell_rows.shape
    head_size = model_width // HEADS
    flat_rows = cell_rows.reshape(row_count * feat_count, model_width)
    packed = jnp.dot(flat_rows, qkv_weight, preferred_element_type=jnp.float32).astype(jnp.bfloat16)
    packed = packed.reshape(row_count, feat_count, 3, HEADS, head_size)
    scores = jnp.einsum(
        "rqhd,rkhd->rhqk", packed[:, :, 0], packed[:, :, 1], preferred_element_type=jnp.float32
    ) / math.sqrt(head_size)
    row_top = jnp.max(scores, axis=-1, keepdims=True)
    weights_exp = jnp.exp(scores - row_top)
    weights = (weights_exp / jnp.sum(weights_exp, axis=-1, keepdims=True)).astype(jnp.bfloat16)
    attended = jnp.einsum(
        "rhqk,rkhd->rqhd", weights, packed[:, :, 2], preferred_element_type=jnp.float32
    ).astype(jnp.bfloat16)
    branch = jnp.dot(
        attended.reshape(row_count * feat_count, model_width),
        out_weight,
        preferred_element_type=jnp.float32,
    )
    settled = layer_norm(flat_rows.astype(jnp.float32) + branch, norm_gain, norm_bias)
    return settled.astype(jnp.bfloat16).reshape(row_count, feat_count, model_width)


def item_attention(query_rows, key_rows, key_marks, item_qkv):
    query_count, model_width = query_rows.shape
    key_count = key_rows.shape[0]
    head_size = model_width // HEADS
    queries = jnp.dot(
        query_rows, item_qkv[:, :model_width], preferred_element_type=jnp.float32
    ).astype(jnp.bfloat16)
    queries = queries.reshape(query_count, HEADS, head_size)
    key_values = jnp.dot(
        key_rows, item_qkv[:, model_width:], preferred_element_type=jnp.float32
    ).astype(jnp.bfloat16)
    key_values = key_values.reshape(key_count, 2, HEADS, head_size)
    alive_keys = (key_marks > 0)[None, :]
    head_parts = []
    for head in range(HEADS):
        scores = jnp.dot(
            queries[:, head], key_values[:, 0, head].T, preferred_element_type=jnp.float32
        ) / math.sqrt(head_size)
        masked = jnp.where(alive_keys, scores, NEG)
        row_top = jnp.max(masked, axis=-1, keepdims=True)
        weights_exp = jnp.where(alive_keys, jnp.exp(masked - row_top), 0.0)
        totals = jnp.sum(weights_exp, axis=-1, keepdims=True)
        weighted = jnp.dot(
            weights_exp.astype(jnp.bfloat16), key_values[:, 1, head], preferred_element_type=jnp.float32
        )
        head_parts.append((weighted / totals).astype(jnp.bfloat16))
    return jnp.concatenate(head_parts, axis=1)


def per_device(
    train_cells,
    test_cells,
    train_mask,
    test_mask,
    feat_qkv,
    feat_out,
    feat_gain,
    feat_bias,
    item_qkv,
    item_out,
    item_gain,
    item_bias,
    mlp_in,
    mlp_out,
    mlp_gain,
    mlp_bias,
):
    train_count = train_cells.shape[0]
    row_count = train_count + test_cells.shape[0]
    feat_count, model_width = train_cells.shape[1], train_cells.shape[2]
    both_rows = jnp.concatenate([train_cells, test_cells], axis=0)
    settled = feature_block(both_rows, feat_qkv, feat_out, feat_gain, feat_bias)
    marks = jnp.concatenate([train_mask, test_mask], axis=0).astype(jnp.bfloat16)
    mark_row = jnp.pad(jnp.transpose(marks), ((0, 0), (0, model_width - row_count)))
    outbound = jnp.concatenate(
        [jnp.swapaxes(settled, 0, 1), mark_row[:, None, :]], axis=1
    )
    inbound = lax.all_to_all(outbound, "rows", split_axis=0, concat_axis=0, tiled=True)
    source_count = inbound.shape[0]
    col_rows = inbound[:, :row_count, :]
    col_marks = inbound[:, row_count, :row_count]
    train_rows = col_rows[:, :train_count].reshape(source_count * train_count, model_width)
    train_marks = col_marks[:, :train_count].reshape(source_count * train_count)
    local_keys = train_rows.shape[0]
    key_mark_row = jnp.pad(train_marks, (0, model_width - local_keys))
    gathered = lax.all_gather(
        jnp.concatenate([train_rows, key_mark_row[None, :]], axis=0), "feat", axis=0
    )
    key_rows = gathered[:, :local_keys].reshape(-1, model_width)
    key_marks = gathered[:, local_keys, :local_keys].reshape(-1)

    query_rows = col_rows.reshape(source_count * row_count, model_width)
    attended = item_attention(query_rows, key_rows, key_marks, item_qkv)
    branch = jnp.dot(attended, item_out, preferred_element_type=jnp.float32)
    is_train = (jnp.arange(row_count) < train_count)[None, :]
    keep_gate = jnp.where(is_train, jnp.ones_like(col_marks), col_marks).astype(jnp.float32)
    branch = branch * keep_gate.reshape(-1, 1)
    settled_item = layer_norm(
        query_rows.astype(jnp.float32) + branch, item_gain, item_bias
    ).astype(jnp.bfloat16)
    hidden_units = jax.nn.gelu(
        jnp.dot(settled_item, mlp_in, preferred_element_type=jnp.float32), approximate=False
    ).astype(jnp.bfloat16)
    result_rows = layer_norm(
        settled_item.astype(jnp.float32)
        + jnp.dot(hidden_units, mlp_out, preferred_element_type=jnp.float32),
        mlp_gain,
        mlp_bias,
    ).astype(jnp.bfloat16)
    result_rows = result_rows.reshape(source_count, row_count, model_width)
    returned = lax.all_to_all(result_rows, "rows", split_axis=0, concat_axis=0, tiled=True)
    final = jnp.swapaxes(returned, 0, 1)
    return (final[:train_count], final[train_count:])


def solution(mesh):
    return jax.shard_map(
        per_device,
        mesh=mesh,
        in_specs=(
            P(("rows", "feat"), None, None),
            P(("rows", "feat"), None, None),
            P(("rows", "feat"), None),
            P(("rows", "feat"), None),
            P(),
            P(),
            P(),
            P(),
            P(),
            P(),
            P(),
            P(),
            P(),
            P(),
            P(),
            P(),
        ),
        out_specs=(P(("rows", "feat"), None, None), P(("rows", "feat"), None, None)),
        check_vma=False,
    )
```

```python
import math

import jax
import jax.numpy as jnp
from jax import lax
from jax.experimental import pallas as pl
from jax.sharding import PartitionSpec as P

HEADS = 6


EPS = 1e-05
NEG = -1e30
SQRT_HALF = math.sqrt(0.5)


def layer_norm(values, norm_gain, norm_bias):
    centre = jnp.mean(values, axis=-1, keepdims=True)
    centred = values - centre
    variance = jnp.mean(centred * centred, axis=-1, keepdims=True)
    return centred * lax.rsqrt(variance + EPS) * norm_gain + norm_bias


def feature_block(cell_rows, qkv_weight, out_weight, norm_gain, norm_bias):
    row_count, feat_count, model_width = cell_rows.shape
    head_size = model_width // HEADS
    flat_rows = cell_rows.reshape(row_count * feat_count, model_width)
    packed = jnp.dot(flat_rows, qkv_weight, preferred_element_type=jnp.float32).astype(jnp.bfloat16)
    packed = packed.reshape(row_count, feat_count, 3, HEADS, head_size)
    scores = jnp.einsum(
        "rqhd,rkhd->rhqk", packed[:, :, 0], packed[:, :, 1], preferred_element_type=jnp.float32
    ) / math.sqrt(head_size)
    row_top = jnp.max(scores, axis=-1, keepdims=True)
    weights_exp = jnp.exp(scores - row_top)
    weights = (weights_exp / jnp.sum(weights_exp, axis=-1, keepdims=True)).astype(jnp.bfloat16)
    attended = jnp.einsum(
        "rhqk,rkhd->rqhd", weights, packed[:, :, 2], preferred_element_type=jnp.float32
    ).astype(jnp.bfloat16)
    branch = jnp.dot(
        attended.reshape(row_count * feat_count, model_width),
        out_weight,
        preferred_element_type=jnp.float32,
    )
    settled = layer_norm(flat_rows.astype(jnp.float32) + branch, norm_gain, norm_bias)
    return settled.astype(jnp.bfloat16).reshape(row_count, feat_count, model_width)


def item_attention(query_rows, key_rows, key_marks, item_qkv):
    query_count, model_width = query_rows.shape
    key_count = key_rows.shape[0]
    head_size = model_width // HEADS
    queries = jnp.dot(
        query_rows, item_qkv[:, :model_width], preferred_element_type=jnp.float32
    ).astype(jnp.bfloat16)
    queries = queries.reshape(query_count, HEADS, head_size)
    key_values = jnp.dot(
        key_rows, item_qkv[:, model_width:], preferred_element_type=jnp.float32
    ).astype(jnp.bfloat16)
    key_values = key_values.reshape(key_count, 2, HEADS, head_size)
    scores = jnp.einsum(
        "qhd,khd->hqk", queries, key_values[:, 0], preferred_element_type=jnp.float32
    ) / math.sqrt(head_size)
    alive_keys = (key_marks > 0)[None, None, :]
    masked = jnp.where(alive_keys, scores, NEG)
    row_top = jnp.max(masked, axis=-1, keepdims=True)
    weights_exp = jnp.where(alive_keys, jnp.exp(masked - row_top), 0.0)
    totals = jnp.sum(weights_exp, axis=-1)
    weighted = jnp.einsum(
        "hqk,khd->hqd",
        weights_exp.astype(jnp.bfloat16),
        key_values[:, 1],
        preferred_element_type=jnp.float32,
    )
    attended = (weighted / totals[..., None]).astype(jnp.bfloat16)
    return jnp.transpose(attended, (1, 0, 2)).reshape(query_count, model_width)


def tail_kernel(
    mixed_ref, rows_ref, item_out_ref, item_gain_ref, item_bias_ref,
    mlp_in_ref, mlp_out_ref, mlp_gain_ref, mlp_bias_ref, out_ref,
):
    branch = jnp.dot(mixed_ref[...], item_out_ref[...], preferred_element_type=jnp.float32)
    settled = layer_norm(
        rows_ref[...].astype(jnp.float32) + branch, item_gain_ref[...], item_bias_ref[...]
    ).astype(jnp.bfloat16)
    pre = jnp.dot(settled, mlp_in_ref[...], preferred_element_type=jnp.float32)
    inner = (0.5 * pre * (1.0 + lax.erf(pre * SQRT_HALF))).astype(jnp.bfloat16)
    result = layer_norm(
        settled.astype(jnp.float32)
        + jnp.dot(inner, mlp_out_ref[...], preferred_element_type=jnp.float32),
        mlp_gain_ref[...],
        mlp_bias_ref[...],
    )
    out_ref[...] = result.astype(out_ref.dtype)


def item_tail(mixed, rows, item_out, item_gain, item_bias, mlp_in, mlp_out, mlp_gain, mlp_bias):
    cell_count, model_width = rows.shape
    hidden_width = mlp_in.shape[1]
    as_row = lambda vector: vector.reshape(1, model_width)
    return pl.pallas_call(
        tail_kernel,
        out_shape=jax.ShapeDtypeStruct((cell_count, model_width), jnp.bfloat16),
        cost_estimate=pl.CostEstimate(
            flops=2 * cell_count * model_width * (model_width + 2 * hidden_width),
            transcendentals=cell_count * hidden_width,
            bytes_accessed=2 * (3 * cell_count * model_width
                                + model_width * (model_width + 2 * hidden_width)),
        ),
    )(
        mixed, rows, item_out, as_row(item_gain), as_row(item_bias),
        mlp_in, mlp_out, as_row(mlp_gain), as_row(mlp_bias),
    )


def per_device(
    train_cells,
    test_cells,
    train_mask,
    test_mask,
    feat_qkv,
    feat_out,
    feat_gain,
    feat_bias,
    item_qkv,
    item_out,
    item_gain,
    item_bias,
    mlp_in,
    mlp_out,
    mlp_gain,
    mlp_bias,
):
    train_count = train_cells.shape[0]
    row_count = train_count + test_cells.shape[0]
    feat_count, model_width = train_cells.shape[1], train_cells.shape[2]
    both_rows = jnp.concatenate([train_cells, test_cells], axis=0)
    settled = feature_block(both_rows, feat_qkv, feat_out, feat_gain, feat_bias)
    marks = jnp.concatenate([train_mask, test_mask], axis=0).astype(jnp.bfloat16)
    mark_row = jnp.pad(jnp.transpose(marks), ((0, 0), (0, model_width - row_count)))
    outbound = jnp.concatenate(
        [jnp.swapaxes(settled, 0, 1), mark_row[:, None, :]], axis=1
    )
    inbound = lax.all_to_all(outbound, "rows", split_axis=0, concat_axis=0, tiled=True)
    source_count = inbound.shape[0]
    col_rows = inbound[:, :row_count, :]
    col_marks = inbound[:, row_count, :row_count]
    train_rows = col_rows[:, :train_count].reshape(source_count * train_count, model_width)
    train_marks = col_marks[:, :train_count].reshape(source_count * train_count)
    local_keys = train_rows.shape[0]
    key_mark_row = jnp.pad(train_marks, (0, model_width - local_keys))
    gathered = lax.all_gather(
        jnp.concatenate([train_rows, key_mark_row[None, :]], axis=0), "feat", axis=0
    )
    key_rows = gathered[:, :local_keys].reshape(-1, model_width)
    key_marks = gathered[:, local_keys, :local_keys].reshape(-1)

    query_rows = col_rows.reshape(source_count * row_count, model_width)
    attended = item_attention(query_rows, key_rows, key_marks, item_qkv)
    is_train = (jnp.arange(row_count) < train_count)[None, :]
    keep_gate = jnp.where(is_train, jnp.ones_like(col_marks), col_marks)
    gated = attended * keep_gate.reshape(-1, 1)
    result_rows = item_tail(
        gated, query_rows, item_out, item_gain, item_bias, mlp_in, mlp_out, mlp_gain, mlp_bias
    )
    result_rows = result_rows.reshape(source_count, row_count, model_width)
    returned = lax.all_to_all(result_rows, "rows", split_axis=0, concat_axis=0, tiled=True)
    final = jnp.swapaxes(returned, 0, 1)
    return (final[:train_count], final[train_count:])


def solution(mesh):
    return jax.shard_map(
        per_device,
        mesh=mesh,
        in_specs=(
            P(("rows", "feat"), None, None),
            P(("rows", "feat"), None, None),
            P(("rows", "feat"), None),
            P(("rows", "feat"), None),
            P(),
            P(),
            P(),
            P(),
            P(),
            P(),
            P(),
            P(),
            P(),
            P(),
            P(),
            P(),
        ),
        out_specs=(P(("rows", "feat"), None, None), P(("rows", "feat"), None, None)),
        check_vma=False,
    )
```

```python
import math

import jax
import jax.numpy as jnp
from jax import lax
from jax.experimental import pallas as pl
from jax.sharding import PartitionSpec as P

HEADS = 6


EPS = 1e-05
NEG = -1e30
SQRT_HALF = math.sqrt(0.5)


def layer_norm(values, norm_gain, norm_bias):
    centre = jnp.mean(values, axis=-1, keepdims=True)
    centred = values - centre
    variance = jnp.mean(centred * centred, axis=-1, keepdims=True)
    return centred * lax.rsqrt(variance + EPS) * norm_gain + norm_bias


def feature_block(cell_rows, qkv_weight, out_weight, norm_gain, norm_bias):
    row_count, feat_count, model_width = cell_rows.shape
    head_size = model_width // HEADS
    flat_rows = cell_rows.reshape(row_count * feat_count, model_width)
    packed = jnp.dot(flat_rows, qkv_weight, preferred_element_type=jnp.float32).astype(jnp.bfloat16)
    packed = packed.reshape(row_count, feat_count, 3, HEADS, head_size)
    scores = jnp.einsum(
        "rqhd,rkhd->rhqk", packed[:, :, 0], packed[:, :, 1], preferred_element_type=jnp.float32
    ) / math.sqrt(head_size)
    row_top = jnp.max(scores, axis=-1, keepdims=True)
    weights_exp = jnp.exp(scores - row_top)
    weights = (weights_exp / jnp.sum(weights_exp, axis=-1, keepdims=True)).astype(jnp.bfloat16)
    attended = jnp.einsum(
        "rhqk,rkhd->rqhd", weights, packed[:, :, 2], preferred_element_type=jnp.float32
    ).astype(jnp.bfloat16)
    branch = jnp.dot(
        attended.reshape(row_count * feat_count, model_width),
        out_weight,
        preferred_element_type=jnp.float32,
    )
    settled = layer_norm(flat_rows.astype(jnp.float32) + branch, norm_gain, norm_bias)
    return settled.astype(jnp.bfloat16).reshape(row_count, feat_count, model_width)


def item_attention(query_rows, key_rows, key_marks, row_gate, item_qkv):
    query_count, model_width = query_rows.shape
    key_count = key_rows.shape[0]
    head_size = model_width // HEADS
    queries = jnp.dot(
        query_rows, item_qkv[:, :model_width], preferred_element_type=jnp.float32
    ).astype(jnp.bfloat16)
    queries = queries.reshape(query_count, HEADS, head_size)
    key_values = jnp.dot(
        key_rows, item_qkv[:, model_width:], preferred_element_type=jnp.float32
    ).astype(jnp.bfloat16)
    key_values = key_values.reshape(key_count, 2, HEADS, head_size)
    scores = jnp.einsum(
        "qhd,khd->hqk", queries, key_values[:, 0], preferred_element_type=jnp.float32
    ) / math.sqrt(head_size)
    alive_keys = (key_marks > 0)[None, None, :]
    masked = jnp.where(alive_keys, scores, NEG)
    row_top = jnp.max(masked, axis=-1, keepdims=True)
    weights_exp = jnp.where(alive_keys, jnp.exp(masked - row_top), 0.0)
    totals = jnp.sum(weights_exp, axis=-1)
    weighted = jnp.einsum(
        "hqk,khd->hqd",
        weights_exp.astype(jnp.bfloat16),
        key_values[:, 1],
        preferred_element_type=jnp.float32,
    )
    attended = ((weighted * row_gate[None, :, None]) / totals[..., None]).astype(jnp.bfloat16)
    return jnp.transpose(attended, (1, 0, 2)).reshape(query_count, model_width)


def tail_kernel(
    mixed_ref, rows_ref, item_out_ref, item_gain_ref, item_bias_ref,
    mlp_in_ref, mlp_out_ref, mlp_gain_ref, mlp_bias_ref, out_ref,
):
    branch = jnp.dot(mixed_ref[...], item_out_ref[...], preferred_element_type=jnp.float32)
    settled = layer_norm(
        rows_ref[...].astype(jnp.float32) + branch, item_gain_ref[...], item_bias_ref[...]
    ).astype(jnp.bfloat16)
    pre = jnp.dot(settled, mlp_in_ref[...], preferred_element_type=jnp.float32)
    inner = (0.5 * pre * (1.0 + lax.erf(pre * SQRT_HALF))).astype(jnp.bfloat16)
    result = layer_norm(
        settled.astype(jnp.float32)
        + jnp.dot(inner, mlp_out_ref[...], preferred_element_type=jnp.float32),
        mlp_gain_ref[...],
        mlp_bias_ref[...],
    )
    out_ref[...] = result.astype(out_ref.dtype)


def item_tail(mixed, rows, item_out, item_gain, item_bias, mlp_in, mlp_out, mlp_gain, mlp_bias):
    cell_count, model_width = rows.shape
    hidden_width = mlp_in.shape[1]
    as_row = lambda vector: vector.reshape(1, model_width)
    return pl.pallas_call(
        tail_kernel,
        out_shape=jax.ShapeDtypeStruct((cell_count, model_width), jnp.bfloat16),
        cost_estimate=pl.CostEstimate(
            flops=2 * cell_count * model_width * (model_width + 2 * hidden_width),
            transcendentals=cell_count * hidden_width,
            bytes_accessed=2 * (3 * cell_count * model_width
                                + model_width * (model_width + 2 * hidden_width)),
        ),
    )(
        mixed, rows, item_out, as_row(item_gain), as_row(item_bias),
        mlp_in, mlp_out, as_row(mlp_gain), as_row(mlp_bias),
    )


def per_device(
    train_cells,
    test_cells,
    train_mask,
    test_mask,
    feat_qkv,
    feat_out,
    feat_gain,
    feat_bias,
    item_qkv,
    item_out,
    item_gain,
    item_bias,
    mlp_in,
    mlp_out,
    mlp_gain,
    mlp_bias,
):
    train_count = train_cells.shape[0]
    row_count = train_count + test_cells.shape[0]
    feat_count, model_width = train_cells.shape[1], train_cells.shape[2]
    both_rows = jnp.concatenate([train_cells, test_cells], axis=0)
    settled = feature_block(both_rows, feat_qkv, feat_out, feat_gain, feat_bias)
    marks = jnp.concatenate([train_mask, test_mask], axis=0).astype(jnp.bfloat16)
    mark_row = jnp.pad(jnp.transpose(marks), ((0, 0), (0, model_width - row_count)))
    outbound = jnp.concatenate(
        [jnp.swapaxes(settled, 0, 1), mark_row[:, None, :]], axis=1
    )
    inbound = lax.all_to_all(outbound, "rows", split_axis=0, concat_axis=0, tiled=True)
    source_count = inbound.shape[0]
    col_rows = inbound[:, :row_count, :]
    col_marks = inbound[:, row_count, :row_count]
    train_rows = col_rows[:, :train_count].reshape(source_count * train_count, model_width)
    train_marks = col_marks[:, :train_count].reshape(source_count * train_count)
    local_keys = train_rows.shape[0]
    key_mark_row = jnp.pad(train_marks, (0, model_width - local_keys))
    gathered = lax.all_gather(
        jnp.concatenate([train_rows, key_mark_row[None, :]], axis=0), "feat", axis=0
    )
    key_rows = gathered[:, :local_keys].reshape(-1, model_width)
    key_marks = gathered[:, local_keys, :local_keys].reshape(-1)

    query_rows = col_rows.reshape(source_count * row_count, model_width)
    is_train = (jnp.arange(row_count) < train_count)[None, :]
    keep_gate = jnp.where(is_train, jnp.ones_like(col_marks), col_marks).astype(jnp.float32)
    gated = item_attention(query_rows, key_rows, key_marks, keep_gate.reshape(-1), item_qkv)
    result_rows = item_tail(
        gated, query_rows, item_out, item_gain, item_bias, mlp_in, mlp_out, mlp_gain, mlp_bias
    )
    result_rows = result_rows.reshape(source_count, row_count, model_width)
    returned = lax.all_to_all(result_rows, "rows", split_axis=0, concat_axis=0, tiled=True)
    final = jnp.swapaxes(returned, 0, 1)
    return (final[:train_count], final[train_count:])


def solution(mesh):
    return jax.shard_map(
        per_device,
        mesh=mesh,
        in_specs=(
            P(("rows", "feat"), None, None),
            P(("rows", "feat"), None, None),
            P(("rows", "feat"), None),
            P(("rows", "feat"), None),
            P(),
            P(),
            P(),
            P(),
            P(),
            P(),
            P(),
            P(),
            P(),
            P(),
            P(),
            P(),
        ),
        out_specs=(P(("rows", "feat"), None, None), P(("rows", "feat"), None, None)),
        check_vma=False,
    )
```

```python
import math

import jax
import jax.numpy as jnp
from jax import lax
from jax.experimental import pallas as pl
from jax.sharding import PartitionSpec as P

HEADS = 6


EPS = 1e-05
NEG = -1e30
SQRT_HALF = math.sqrt(0.5)


def layer_norm(values, norm_gain, norm_bias):
    centre = jnp.mean(values, axis=-1, keepdims=True)
    centred = values - centre
    variance = jnp.mean(centred * centred, axis=-1, keepdims=True)
    return centred * lax.rsqrt(variance + EPS) * norm_gain + norm_bias


def feature_block(cell_rows, qkv_weight, out_weight, norm_gain, norm_bias):
    row_count, feat_count, model_width = cell_rows.shape
    head_size = model_width // HEADS
    flat_rows = cell_rows.reshape(row_count * feat_count, model_width)
    packed = jnp.dot(flat_rows, qkv_weight, preferred_element_type=jnp.float32).astype(jnp.bfloat16)
    packed = packed.reshape(row_count, feat_count, 3, HEADS, head_size)
    scores = jnp.einsum(
        "rqhd,rkhd->rhqk", packed[:, :, 0], packed[:, :, 1], preferred_element_type=jnp.float32
    ) / math.sqrt(head_size)
    row_top = jnp.max(scores, axis=-1, keepdims=True)
    weights_exp = jnp.exp(scores - row_top)
    weights = (weights_exp / jnp.sum(weights_exp, axis=-1, keepdims=True)).astype(jnp.bfloat16)
    attended = jnp.einsum(
        "rhqk,rkhd->rqhd", weights, packed[:, :, 2], preferred_element_type=jnp.float32
    ).astype(jnp.bfloat16)
    branch = jnp.dot(
        attended.reshape(row_count * feat_count, model_width),
        out_weight,
        preferred_element_type=jnp.float32,
    )
    settled = layer_norm(flat_rows.astype(jnp.float32) + branch, norm_gain, norm_bias)
    return settled.astype(jnp.bfloat16).reshape(row_count, feat_count, model_width)


def item_attention(query_rows, key_rows, key_marks, row_gate, item_qkv):
    query_count, model_width = query_rows.shape
    key_count = key_rows.shape[0]
    head_size = model_width // HEADS
    queries = jnp.dot(
        query_rows, item_qkv[:, :model_width], preferred_element_type=jnp.float32
    ).astype(jnp.bfloat16)
    queries = queries.reshape(query_count, HEADS, head_size)
    key_values = jnp.dot(
        key_rows, item_qkv[:, model_width:], preferred_element_type=jnp.float32
    ).astype(jnp.bfloat16)
    key_values = key_values.reshape(key_count, 2, HEADS, head_size)
    scores = jnp.einsum(
        "qhd,khd->hqk", queries, key_values[:, 0], preferred_element_type=jnp.float32
    ) / math.sqrt(head_size)
    alive_keys = (key_marks > 0)[None, None, :]
    masked = jnp.where(alive_keys, scores, NEG)
    row_top = jnp.max(masked, axis=-1, keepdims=True)
    weights_exp = jnp.where(alive_keys, jnp.exp(masked - row_top), 0.0)
    totals = jnp.sum(weights_exp, axis=-1)
    weighted = jnp.einsum(
        "hqk,khd->hqd",
        weights_exp.astype(jnp.bfloat16),
        key_values[:, 1],
        preferred_element_type=jnp.float32,
    )
    attended = ((weighted * row_gate[None, :, None]) / totals[..., None]).astype(jnp.bfloat16)
    return jnp.transpose(attended, (0, 2, 1)).reshape(model_width, query_count)


def tail_kernel(
    mixed_ref, rows_ref, item_out_ref, item_gain_ref, item_bias_ref,
    mlp_in_ref, mlp_out_ref, mlp_gain_ref, mlp_bias_ref, out_ref,
):
    branch = lax.dot_general(
        mixed_ref[...], item_out_ref[...], (((0,), (0,)), ((), ())),
        preferred_element_type=jnp.float32,
    )
    settled = layer_norm(
        rows_ref[...].astype(jnp.float32) + branch, item_gain_ref[...], item_bias_ref[...]
    ).astype(jnp.bfloat16)
    pre = jnp.dot(settled, mlp_in_ref[...], preferred_element_type=jnp.float32)
    inner = (0.5 * pre * (1.0 + lax.erf(pre * SQRT_HALF))).astype(jnp.bfloat16)
    result = layer_norm(
        settled.astype(jnp.float32)
        + jnp.dot(inner, mlp_out_ref[...], preferred_element_type=jnp.float32),
        mlp_gain_ref[...],
        mlp_bias_ref[...],
    )
    out_ref[...] = result.astype(out_ref.dtype)


def item_tail(mixed, rows, item_out, item_gain, item_bias, mlp_in, mlp_out, mlp_gain, mlp_bias):
    cell_count, model_width = rows.shape
    hidden_width = mlp_in.shape[1]
    as_row = lambda vector: vector.reshape(1, model_width)
    return pl.pallas_call(
        tail_kernel,
        out_shape=jax.ShapeDtypeStruct((cell_count, model_width), jnp.bfloat16),
        cost_estimate=pl.CostEstimate(
            flops=2 * cell_count * model_width * (model_width + 2 * hidden_width),
            transcendentals=cell_count * hidden_width,
            bytes_accessed=2 * (3 * cell_count * model_width
                                + model_width * (model_width + 2 * hidden_width)),
        ),
    )(
        mixed, rows, item_out, as_row(item_gain), as_row(item_bias),
        mlp_in, mlp_out, as_row(mlp_gain), as_row(mlp_bias),
    )


def per_device(
    train_cells,
    test_cells,
    train_mask,
    test_mask,
    feat_qkv,
    feat_out,
    feat_gain,
    feat_bias,
    item_qkv,
    item_out,
    item_gain,
    item_bias,
    mlp_in,
    mlp_out,
    mlp_gain,
    mlp_bias,
):
    train_count = train_cells.shape[0]
    row_count = train_count + test_cells.shape[0]
    feat_count, model_width = train_cells.shape[1], train_cells.shape[2]
    both_rows = jnp.concatenate([train_cells, test_cells], axis=0)
    settled = feature_block(both_rows, feat_qkv, feat_out, feat_gain, feat_bias)
    marks = jnp.concatenate([train_mask, test_mask], axis=0).astype(jnp.bfloat16)
    mark_row = jnp.pad(jnp.transpose(marks), ((0, 0), (0, model_width - row_count)))
    outbound = jnp.concatenate(
        [jnp.swapaxes(settled, 0, 1), mark_row[:, None, :]], axis=1
    )
    inbound = lax.all_to_all(outbound, "rows", split_axis=0, concat_axis=0, tiled=True)
    source_count = inbound.shape[0]
    col_rows = inbound[:, :row_count, :]
    col_marks = inbound[:, row_count, :row_count]
    train_rows = col_rows[:, :train_count].reshape(source_count * train_count, model_width)
    train_marks = col_marks[:, :train_count].reshape(source_count * train_count)
    local_keys = train_rows.shape[0]
    key_mark_row = jnp.pad(train_marks, (0, model_width - local_keys))
    gathered = lax.all_gather(
        jnp.concatenate([train_rows, key_mark_row[None, :]], axis=0), "feat", axis=0
    )
    key_rows = gathered[:, :local_keys].reshape(-1, model_width)
    key_marks = gathered[:, local_keys, :local_keys].reshape(-1)

    query_rows = col_rows.reshape(source_count * row_count, model_width)
    is_train = (jnp.arange(row_count) < train_count)[None, :]
    keep_gate = jnp.where(is_train, jnp.ones_like(col_marks), col_marks).astype(jnp.float32)
    gated = item_attention(query_rows, key_rows, key_marks, keep_gate.reshape(-1), item_qkv)
    result_rows = item_tail(
        gated, query_rows, item_out, item_gain, item_bias, mlp_in, mlp_out, mlp_gain, mlp_bias
    )
    result_rows = result_rows.reshape(source_count, row_count, model_width)
    returned = lax.all_to_all(result_rows, "rows", split_axis=0, concat_axis=0, tiled=True)
    final = jnp.swapaxes(returned, 0, 1)
    return (final[:train_count], final[train_count:])


def solution(mesh):
    return jax.shard_map(
        per_device,
        mesh=mesh,
        in_specs=(
            P(("rows", "feat"), None, None),
            P(("rows", "feat"), None, None),
            P(("rows", "feat"), None),
            P(("rows", "feat"), None),
            P(),
            P(),
            P(),
            P(),
            P(),
            P(),
            P(),
            P(),
            P(),
            P(),
            P(),
            P(),
        ),
        out_specs=(P(("rows", "feat"), None, None), P(("rows", "feat"), None, None)),
        check_vma=False,
    )
```

```python
import math

import jax
import jax.numpy as jnp
from jax import lax
from jax.experimental import pallas as pl
from jax.sharding import PartitionSpec as P

HEADS = 6


EPS = 1e-05
NEG = -1e30
SQRT_HALF = math.sqrt(0.5)


def layer_norm(values, norm_gain, norm_bias):
    centre = jnp.mean(values, axis=-1, keepdims=True)
    centred = values - centre
    variance = jnp.mean(centred * centred, axis=-1, keepdims=True)
    return centred * lax.rsqrt(variance + EPS) * norm_gain + norm_bias


def feature_block(cell_rows, qkv_weight, out_weight, norm_gain, norm_bias):
    row_count, feat_count, model_width = cell_rows.shape
    head_size = model_width // HEADS
    flat_rows = cell_rows.reshape(row_count * feat_count, model_width)
    packed = jnp.dot(flat_rows, qkv_weight, preferred_element_type=jnp.float32).astype(jnp.bfloat16)
    packed = packed.reshape(row_count, feat_count, 3, HEADS, head_size)
    scores = jnp.einsum(
        "rqhd,rkhd->rhqk", packed[:, :, 0], packed[:, :, 1], preferred_element_type=jnp.float32
    ) / math.sqrt(head_size)
    row_top = jnp.max(scores, axis=-1, keepdims=True)
    weights_exp = jnp.exp(scores - row_top)
    weights = (weights_exp / jnp.sum(weights_exp, axis=-1, keepdims=True)).astype(jnp.bfloat16)
    attended = jnp.einsum(
        "rhqk,rkhd->rqhd", weights, packed[:, :, 2], preferred_element_type=jnp.float32
    ).astype(jnp.bfloat16)
    branch = jnp.dot(
        attended.reshape(row_count * feat_count, model_width),
        out_weight,
        preferred_element_type=jnp.float32,
    )
    settled = layer_norm(flat_rows.astype(jnp.float32) + branch, norm_gain, norm_bias)
    return settled.astype(jnp.bfloat16).reshape(row_count, feat_count, model_width)


def item_attention(query_rows, key_rows, key_marks, row_gate, item_qkv):
    query_count, model_width = query_rows.shape
    key_count = key_rows.shape[0]
    head_size = model_width // HEADS
    queries = jnp.dot(
        query_rows, item_qkv[:, :model_width], preferred_element_type=jnp.float32
    ).astype(jnp.bfloat16)
    queries = queries.reshape(query_count, HEADS, head_size)
    key_values = jnp.dot(
        key_rows, item_qkv[:, model_width:], preferred_element_type=jnp.float32
    ).astype(jnp.bfloat16)
    key_values = key_values.reshape(key_count, 2, HEADS, head_size)
    scores = jnp.einsum(
        "qhd,khd->hqk", queries, key_values[:, 0], preferred_element_type=jnp.float32
    ) / math.sqrt(head_size)
    alive_keys = (key_marks > 0)[None, None, :]
    masked = jnp.where(alive_keys, scores, NEG)
    row_top = jnp.max(masked, axis=-1, keepdims=True)
    weights_exp = jnp.where(alive_keys, jnp.exp(masked - row_top), 0.0)
    totals = jnp.sum(weights_exp, axis=-1)
    weighted = jnp.einsum(
        "hqk,khd->hqd",
        weights_exp.astype(jnp.bfloat16),
        key_values[:, 1],
        preferred_element_type=jnp.float32,
    )
    attended = ((weighted * row_gate[None, :, None]) / totals[..., None]).astype(jnp.bfloat16)
    return jnp.transpose(attended, (0, 2, 1)).reshape(model_width, query_count)


def tail_kernel(
    mixed_ref, rows_ref, item_out_ref, item_gain_ref, item_bias_ref,
    mlp_in_ref, mlp_out_ref, mlp_gain_ref, mlp_bias_ref, out_ref,
):
    branch = lax.dot_general(
        mixed_ref[...], item_out_ref[...], (((0,), (0,)), ((), ())),
        preferred_element_type=jnp.float32,
    )
    settled = layer_norm(
        rows_ref[...].astype(jnp.float32) + branch, item_gain_ref[...], item_bias_ref[...]
    ).astype(jnp.bfloat16)
    pre = jnp.dot(settled, mlp_in_ref[...], preferred_element_type=jnp.float32)
    inner = (0.5 * pre * (1.0 + lax.erf(pre * SQRT_HALF))).astype(jnp.bfloat16)
    result = layer_norm(
        settled.astype(jnp.float32)
        + jnp.dot(inner, mlp_out_ref[...], preferred_element_type=jnp.float32),
        mlp_gain_ref[...],
        mlp_bias_ref[...],
    )
    source_count, row_count = out_ref.shape[0], out_ref.shape[1]
    for source in range(source_count):
        out_ref[source] = result[source * row_count:(source + 1) * row_count].astype(out_ref.dtype)


def item_tail(
    mixed, rows, item_out, item_gain, item_bias, mlp_in, mlp_out, mlp_gain, mlp_bias, source_count
):
    cell_count, model_width = rows.shape
    hidden_width = mlp_in.shape[1]
    as_row = lambda vector: vector.reshape(1, model_width)
    return pl.pallas_call(
        tail_kernel,
        out_shape=jax.ShapeDtypeStruct(
            (source_count, cell_count // source_count, model_width), jnp.bfloat16
        ),
        cost_estimate=pl.CostEstimate(
            flops=2 * cell_count * model_width * (model_width + 2 * hidden_width),
            transcendentals=cell_count * hidden_width,
            bytes_accessed=2 * (3 * cell_count * model_width
                                + model_width * (model_width + 2 * hidden_width)),
        ),
    )(
        mixed, rows, item_out, as_row(item_gain), as_row(item_bias),
        mlp_in, mlp_out, as_row(mlp_gain), as_row(mlp_bias),
    )


def per_device(
    train_cells,
    test_cells,
    train_mask,
    test_mask,
    feat_qkv,
    feat_out,
    feat_gain,
    feat_bias,
    item_qkv,
    item_out,
    item_gain,
    item_bias,
    mlp_in,
    mlp_out,
    mlp_gain,
    mlp_bias,
):
    train_count = train_cells.shape[0]
    row_count = train_count + test_cells.shape[0]
    feat_count, model_width = train_cells.shape[1], train_cells.shape[2]
    both_rows = jnp.concatenate([train_cells, test_cells], axis=0)
    settled = feature_block(both_rows, feat_qkv, feat_out, feat_gain, feat_bias)
    marks = jnp.concatenate([train_mask, test_mask], axis=0).astype(jnp.bfloat16)
    mark_row = jnp.pad(jnp.transpose(marks), ((0, 0), (0, model_width - row_count)))
    outbound = jnp.concatenate(
        [jnp.swapaxes(settled, 0, 1), mark_row[:, None, :]], axis=1
    )
    inbound = lax.all_to_all(outbound, "rows", split_axis=0, concat_axis=0, tiled=True)
    source_count = inbound.shape[0]
    col_rows = inbound[:, :row_count, :]
    col_marks = inbound[:, row_count, :row_count]
    train_rows = col_rows[:, :train_count].reshape(source_count * train_count, model_width)
    train_marks = col_marks[:, :train_count].reshape(source_count * train_count)
    local_keys = train_rows.shape[0]
    key_mark_row = jnp.pad(train_marks, (0, model_width - local_keys))
    gathered = lax.all_gather(
        jnp.concatenate([train_rows, key_mark_row[None, :]], axis=0), "feat", axis=0
    )
    key_rows = gathered[:, :local_keys].reshape(-1, model_width)
    key_marks = gathered[:, local_keys, :local_keys].reshape(-1)

    query_rows = col_rows.reshape(source_count * row_count, model_width)
    is_train = (jnp.arange(row_count) < train_count)[None, :]
    keep_gate = jnp.where(is_train, jnp.ones_like(col_marks), col_marks).astype(jnp.float32)
    gated = item_attention(query_rows, key_rows, key_marks, keep_gate.reshape(-1), item_qkv)
    result_rows = item_tail(
        gated, query_rows, item_out, item_gain, item_bias, mlp_in, mlp_out, mlp_gain, mlp_bias,
        source_count,
    )
    returned = lax.all_to_all(result_rows, "rows", split_axis=0, concat_axis=0, tiled=True)
    final = jnp.swapaxes(returned, 0, 1)
    return (final[:train_count], final[train_count:])


def solution(mesh):
    return jax.shard_map(
        per_device,
        mesh=mesh,
        in_specs=(
            P(("rows", "feat"), None, None),
            P(("rows", "feat"), None, None),
            P(("rows", "feat"), None),
            P(("rows", "feat"), None),
            P(),
            P(),
            P(),
            P(),
            P(),
            P(),
            P(),
            P(),
            P(),
            P(),
            P(),
            P(),
        ),
        out_specs=(P(("rows", "feat"), None, None), P(("rows", "feat"), None, None)),
        check_vma=False,
    )
```

```python
import math

import jax
import jax.numpy as jnp
from jax import lax
from jax.experimental import pallas as pl
from jax.sharding import PartitionSpec as P

HEADS = 6


EPS = 1e-05
NEG = -1e30
SQRT_HALF = math.sqrt(0.5)


def layer_norm(values, norm_gain, norm_bias):
    centre = jnp.mean(values, axis=-1, keepdims=True)
    centred = values - centre
    variance = jnp.mean(centred * centred, axis=-1, keepdims=True)
    return centred * lax.rsqrt(variance + EPS) * norm_gain + norm_bias


def feature_block(cell_rows, qkv_weight, out_weight, norm_gain, norm_bias):
    row_count, feat_count, model_width = cell_rows.shape
    head_size = model_width // HEADS
    flat_rows = cell_rows.reshape(row_count * feat_count, model_width)
    packed = jnp.dot(flat_rows, qkv_weight, preferred_element_type=jnp.float32).astype(jnp.bfloat16)
    packed = packed.reshape(row_count, feat_count, 3, HEADS, head_size)
    scores = jnp.einsum(
        "rqhd,rkhd->rhqk", packed[:, :, 0], packed[:, :, 1], preferred_element_type=jnp.float32
    ) / math.sqrt(head_size)
    row_top = jnp.max(scores, axis=-1, keepdims=True)
    weights_exp = jnp.exp(scores - row_top)
    weights = (weights_exp / jnp.sum(weights_exp, axis=-1, keepdims=True)).astype(jnp.bfloat16)
    attended = jnp.einsum(
        "rhqk,rkhd->rqhd", weights, packed[:, :, 2], preferred_element_type=jnp.float32
    ).astype(jnp.bfloat16)
    branch = jnp.dot(
        attended.reshape(row_count * feat_count, model_width),
        out_weight,
        preferred_element_type=jnp.float32,
    )
    settled = layer_norm(flat_rows.astype(jnp.float32) + branch, norm_gain, norm_bias)
    return settled.astype(jnp.bfloat16).reshape(row_count, feat_count, model_width)


def item_attention(query_rows, key_rows, key_marks, row_gate, item_qkv):
    query_count, model_width = query_rows.shape
    key_count = key_rows.shape[0]
    head_size = model_width // HEADS
    queries = jnp.dot(
        query_rows, item_qkv[:, :model_width], preferred_element_type=jnp.float32
    ).astype(jnp.bfloat16)
    queries = queries.reshape(query_count, HEADS, head_size)
    key_values = jnp.dot(
        key_rows, item_qkv[:, model_width:], preferred_element_type=jnp.float32
    ).astype(jnp.bfloat16)
    key_values = key_values.reshape(key_count, 2, HEADS, head_size)
    scores = jnp.einsum(
        "qhd,khd->hqk", queries, key_values[:, 0], preferred_element_type=jnp.float32
    ) / math.sqrt(head_size)
    alive_keys = (key_marks > 0)[None, None, :]
    masked = jnp.where(alive_keys, scores, NEG)
    row_top = jnp.max(masked, axis=-1, keepdims=True)
    weights_exp = jnp.where(alive_keys, jnp.exp(masked - row_top), 0.0)
    totals = jnp.sum(weights_exp, axis=-1)
    weighted = jnp.einsum(
        "hqk,khd->hqd",
        weights_exp.astype(jnp.bfloat16),
        key_values[:, 1],
        preferred_element_type=jnp.float32,
    )
    attended = ((weighted * row_gate[None, :, None]) / totals[..., None]).astype(jnp.bfloat16)
    return jnp.transpose(attended, (0, 2, 1)).reshape(model_width, query_count)


def tail_kernel(
    mixed_ref, rows_ref, item_out_ref, item_gain_ref, item_bias_ref,
    mlp_in_ref, mlp_out_ref, mlp_gain_ref, mlp_bias_ref, out_ref,
):
    branch = lax.dot_general(
        mixed_ref[...], item_out_ref[...], (((0,), (0,)), ((), ())),
        preferred_element_type=jnp.float32,
    )
    settled = layer_norm(
        rows_ref[...].astype(jnp.float32) + branch, item_gain_ref[...], item_bias_ref[...]
    ).astype(jnp.bfloat16)
    pre = jnp.dot(settled, mlp_in_ref[...], preferred_element_type=jnp.float32)
    inner = (0.5 * pre * (1.0 + lax.erf(pre * SQRT_HALF))).astype(jnp.bfloat16)
    result = layer_norm(
        settled.astype(jnp.float32)
        + jnp.dot(inner, mlp_out_ref[...], preferred_element_type=jnp.float32),
        mlp_gain_ref[...],
        mlp_bias_ref[...],
    )
    source_count, row_count = out_ref.shape[0], out_ref.shape[1]
    for source in range(source_count):
        out_ref[source] = result[source * row_count:(source + 1) * row_count].astype(out_ref.dtype)


def item_tail(
    mixed, rows, item_out, item_gain, item_bias, mlp_in, mlp_out, mlp_gain, mlp_bias, source_count
):
    cell_count, model_width = rows.shape
    hidden_width = mlp_in.shape[1]
    as_row = lambda vector: vector.reshape(1, model_width)
    return pl.pallas_call(
        tail_kernel,
        out_shape=jax.ShapeDtypeStruct(
            (source_count, cell_count // source_count, model_width), jnp.bfloat16
        ),
        cost_estimate=pl.CostEstimate(
            flops=2 * cell_count * model_width * (model_width + 2 * hidden_width),
            transcendentals=cell_count * hidden_width,
            bytes_accessed=2 * (3 * cell_count * model_width
                                + model_width * (model_width + 2 * hidden_width)),
        ),
    )(
        mixed, rows, item_out, as_row(item_gain), as_row(item_bias),
        mlp_in, mlp_out, as_row(mlp_gain), as_row(mlp_bias),
    )


def per_device(
    train_cells,
    test_cells,
    train_mask,
    test_mask,
    feat_qkv,
    feat_out,
    feat_gain,
    feat_bias,
    item_qkv,
    item_out,
    item_gain,
    item_bias,
    mlp_in,
    mlp_out,
    mlp_gain,
    mlp_bias,
):
    train_count = train_cells.shape[0]
    row_count = train_count + test_cells.shape[0]
    feat_count, model_width = train_cells.shape[1], train_cells.shape[2]
    both_rows = jnp.concatenate([train_cells, test_cells], axis=0)
    settled = feature_block(both_rows, feat_qkv, feat_out, feat_gain, feat_bias)
    live = jnp.transpose(jnp.concatenate([train_mask, test_mask], axis=0)) > 0
    mark_row = jnp.pad(
        jnp.where(live, 1.0, 0.0).astype(jnp.bfloat16), ((0, 0), (0, model_width - row_count))
    )
    outbound = jnp.concatenate(
        [jnp.swapaxes(settled, 0, 1), mark_row[:, None, :]], axis=1
    )
    inbound = lax.all_to_all(outbound, "rows", split_axis=0, concat_axis=0, tiled=True)
    source_count = inbound.shape[0]
    col_rows = inbound[:, :row_count, :]
    col_marks = inbound[:, row_count, :row_count]
    train_rows = col_rows[:, :train_count].reshape(source_count * train_count, model_width)
    train_marks = col_marks[:, :train_count].reshape(source_count * train_count)
    local_keys = train_rows.shape[0]
    key_mark_row = jnp.pad(train_marks, (0, model_width - local_keys))
    gathered = lax.all_gather(
        jnp.concatenate([train_rows, key_mark_row[None, :]], axis=0), "feat", axis=0
    )
    key_rows = gathered[:, :local_keys].reshape(-1, model_width)
    key_marks = gathered[:, local_keys, :local_keys].reshape(-1)

    query_rows = col_rows.reshape(source_count * row_count, model_width)
    is_train = (jnp.arange(row_count) < train_count)[None, :]
    keep_gate = jnp.where(is_train, jnp.ones_like(col_marks), col_marks).astype(jnp.float32)
    gated = item_attention(query_rows, key_rows, key_marks, keep_gate.reshape(-1), item_qkv)
    result_rows = item_tail(
        gated, query_rows, item_out, item_gain, item_bias, mlp_in, mlp_out, mlp_gain, mlp_bias,
        source_count,
    )
    returned = lax.all_to_all(result_rows, "rows", split_axis=0, concat_axis=0, tiled=True)
    final = jnp.swapaxes(returned, 0, 1)
    return (final[:train_count], final[train_count:])


def solution(mesh):
    return jax.shard_map(
        per_device,
        mesh=mesh,
        in_specs=(
            P(("rows", "feat"), None, None),
            P(("rows", "feat"), None, None),
            P(("rows", "feat"), None),
            P(("rows", "feat"), None),
            P(),
            P(),
            P(),
            P(),
            P(),
            P(),
            P(),
            P(),
            P(),
            P(),
            P(),
            P(),
        ),
        out_specs=(P(("rows", "feat"), None, None), P(("rows", "feat"), None, None)),
        check_vma=False,
    )
```

```python
import math

import jax
import jax.numpy as jnp
from jax import lax
from jax.experimental import pallas as pl
from jax.sharding import PartitionSpec as P

HEADS = 6


EPS = 1e-05
NEG = -1e30
SQRT_HALF = math.sqrt(0.5)


def layer_norm(values, norm_gain, norm_bias):
    centre = jnp.mean(values, axis=-1, keepdims=True)
    centred = values - centre
    variance = jnp.mean(centred * centred, axis=-1, keepdims=True)
    return centred * lax.rsqrt(variance + EPS) * norm_gain + norm_bias


def feature_block(cell_rows, qkv_weight, out_weight, norm_gain, norm_bias):
    row_count, feat_count, model_width = cell_rows.shape
    head_size = model_width // HEADS
    flat_rows = cell_rows.reshape(row_count * feat_count, model_width)
    packed = jnp.dot(flat_rows, qkv_weight, preferred_element_type=jnp.float32).astype(jnp.bfloat16)
    packed = packed.reshape(row_count, feat_count, 3, HEADS, head_size)
    scores = jnp.einsum(
        "rqhd,rkhd->rhqk", packed[:, :, 0], packed[:, :, 1], preferred_element_type=jnp.float32
    ) / math.sqrt(head_size)
    row_top = jnp.max(scores, axis=-1, keepdims=True)
    weights_exp = jnp.exp(scores - row_top)
    weights = (weights_exp / jnp.sum(weights_exp, axis=-1, keepdims=True)).astype(jnp.bfloat16)
    attended = jnp.einsum(
        "rhqk,rkhd->rqhd", weights, packed[:, :, 2], preferred_element_type=jnp.float32
    ).astype(jnp.bfloat16)
    branch = jnp.dot(
        attended.reshape(row_count * feat_count, model_width),
        out_weight,
        preferred_element_type=jnp.float32,
    )
    settled = layer_norm(flat_rows.astype(jnp.float32) + branch, norm_gain, norm_bias)
    return settled.astype(jnp.bfloat16).reshape(row_count, feat_count, model_width)


def item_attention(query_rows, key_rows, key_marks, row_gate, item_qkv):
    query_count, model_width = query_rows.shape
    key_count = key_rows.shape[0]
    head_size = model_width // HEADS
    queries = jnp.dot(
        query_rows, item_qkv[:, :model_width], preferred_element_type=jnp.float32
    ).astype(jnp.bfloat16)
    queries = queries.reshape(query_count, HEADS, head_size)
    key_values = jnp.dot(
        key_rows, item_qkv[:, model_width:], preferred_element_type=jnp.float32
    ).astype(jnp.bfloat16)
    key_values = key_values.reshape(key_count, 2, HEADS, head_size)
    scores = jnp.einsum(
        "qhd,khd->hqk", queries, key_values[:, 0], preferred_element_type=jnp.float32
    ) / math.sqrt(head_size)
    alive_keys = (key_marks > 0)[None, None, :]
    masked = jnp.where(alive_keys, scores, NEG)
    row_top = jnp.max(masked, axis=-1, keepdims=True)
    weights_exp = jnp.exp(masked - row_top)
    totals = jnp.sum(weights_exp, axis=-1)
    weighted = jnp.einsum(
        "hqk,khd->hqd",
        weights_exp.astype(jnp.bfloat16),
        key_values[:, 1],
        preferred_element_type=jnp.float32,
    )
    attended = ((weighted * row_gate[None, :, None]) / totals[..., None]).astype(jnp.bfloat16)
    return jnp.transpose(attended, (0, 2, 1)).reshape(model_width, query_count)


def tail_kernel(
    mixed_ref, rows_ref, item_out_ref, item_gain_ref, item_bias_ref,
    mlp_in_ref, mlp_out_ref, mlp_gain_ref, mlp_bias_ref, out_ref,
):
    branch = lax.dot_general(
        mixed_ref[...], item_out_ref[...], (((0,), (0,)), ((), ())),
        preferred_element_type=jnp.float32,
    )
    settled = layer_norm(
        rows_ref[...].astype(jnp.float32) + branch, item_gain_ref[...], item_bias_ref[...]
    ).astype(jnp.bfloat16)
    pre = jnp.dot(settled, mlp_in_ref[...], preferred_element_type=jnp.float32)
    inner = (0.5 * pre * (1.0 + lax.erf(pre * SQRT_HALF))).astype(jnp.bfloat16)
    result = layer_norm(
        settled.astype(jnp.float32)
        + jnp.dot(inner, mlp_out_ref[...], preferred_element_type=jnp.float32),
        mlp_gain_ref[...],
        mlp_bias_ref[...],
    )
    source_count, row_count = out_ref.shape[0], out_ref.shape[1]
    for source in range(source_count):
        out_ref[source] = result[source * row_count:(source + 1) * row_count].astype(out_ref.dtype)


def item_tail(
    mixed, rows, item_out, item_gain, item_bias, mlp_in, mlp_out, mlp_gain, mlp_bias, source_count
):
    cell_count, model_width = rows.shape
    hidden_width = mlp_in.shape[1]
    as_row = lambda vector: vector.reshape(1, model_width)
    return pl.pallas_call(
        tail_kernel,
        out_shape=jax.ShapeDtypeStruct(
            (source_count, cell_count // source_count, model_width), jnp.bfloat16
        ),
        cost_estimate=pl.CostEstimate(
            flops=2 * cell_count * model_width * (model_width + 2 * hidden_width),
            transcendentals=cell_count * hidden_width,
            bytes_accessed=2 * (3 * cell_count * model_width
                                + model_width * (model_width + 2 * hidden_width)),
        ),
    )(
        mixed, rows, item_out, as_row(item_gain), as_row(item_bias),
        mlp_in, mlp_out, as_row(mlp_gain), as_row(mlp_bias),
    )


def per_device(
    train_cells,
    test_cells,
    train_mask,
    test_mask,
    feat_qkv,
    feat_out,
    feat_gain,
    feat_bias,
    item_qkv,
    item_out,
    item_gain,
    item_bias,
    mlp_in,
    mlp_out,
    mlp_gain,
    mlp_bias,
):
    train_count = train_cells.shape[0]
    row_count = train_count + test_cells.shape[0]
    feat_count, model_width = train_cells.shape[1], train_cells.shape[2]
    both_rows = jnp.concatenate([train_cells, test_cells], axis=0)
    settled = feature_block(both_rows, feat_qkv, feat_out, feat_gain, feat_bias)
    marks = jnp.concatenate([train_mask, test_mask], axis=0).astype(jnp.bfloat16)
    mark_row = jnp.pad(jnp.transpose(marks), ((0, 0), (0, model_width - row_count)))
    outbound = jnp.concatenate(
        [jnp.swapaxes(settled, 0, 1), mark_row[:, None, :]], axis=1
    )
    inbound = lax.all_to_all(outbound, "rows", split_axis=0, concat_axis=0, tiled=True)
    source_count = inbound.shape[0]
    col_rows = inbound[:, :row_count, :]
    col_marks = inbound[:, row_count, :row_count]
    train_rows = col_rows[:, :train_count].reshape(source_count * train_count, model_width)
    train_marks = col_marks[:, :train_count].reshape(source_count * train_count)
    local_keys = train_rows.shape[0]
    key_mark_row = jnp.pad(train_marks, (0, model_width - local_keys))
    gathered = lax.all_gather(
        jnp.concatenate([train_rows, key_mark_row[None, :]], axis=0), "feat", axis=0
    )
    key_rows = gathered[:, :local_keys].reshape(-1, model_width)
    key_marks = gathered[:, local_keys, :local_keys].reshape(-1)

    query_rows = col_rows.reshape(source_count * row_count, model_width)
    is_train = (jnp.arange(row_count) < train_count)[None, :]
    keep_gate = jnp.where(is_train, jnp.ones_like(col_marks), col_marks).astype(jnp.float32)
    gated = item_attention(query_rows, key_rows, key_marks, keep_gate.reshape(-1), item_qkv)
    result_rows = item_tail(
        gated, query_rows, item_out, item_gain, item_bias, mlp_in, mlp_out, mlp_gain, mlp_bias,
        source_count,
    )
    returned = lax.all_to_all(result_rows, "rows", split_axis=0, concat_axis=0, tiled=True)
    final = jnp.swapaxes(returned, 0, 1)
    return (final[:train_count], final[train_count:])


def solution(mesh):
    return jax.shard_map(
        per_device,
        mesh=mesh,
        in_specs=(
            P(("rows", "feat"), None, None),
            P(("rows", "feat"), None, None),
            P(("rows", "feat"), None),
            P(("rows", "feat"), None),
            P(),
            P(),
            P(),
            P(),
            P(),
            P(),
            P(),
            P(),
            P(),
            P(),
            P(),
            P(),
        ),
        out_specs=(P(("rows", "feat"), None, None), P(("rows", "feat"), None, None)),
        check_vma=False,
    )
```
